256 devices in a mesh: dp: 128 (over z, x, y), group: 2 (over core).
Axes of the slice: x: 4, y: 4, z: 8, core: 2. Of those that a mesh axis runs over, the one named last changes fastest.
Arguments:
- queries: bfloat16 [2048, 1024], P(('dp', 'group')), may hold values from -6 to 6
- passage_hidden: bfloat16 [32768, 1024], P('dp'), may hold values from -24 to 24
- out_weight: bfloat16 [1024, 1024], replicated, may hold values from -0.1875 to 0.1875
- neg_owner: int32 [65536, 1], P(('dp', 'group')), may hold values from 0 to 127; in each aligned block of 256 rows (0 to 255, 256 to 511, ...) at most 4 rows name the same one
- neg_local: int32 [2048, 32], P(('dp', 'group')), may hold values from 0 to 255
Outputs:
- weight_grad: float32 [1024, 1024], P('dp')
- query_loss: float32 [2048], P(('dp', 'group'))
The draws below stay inside these ranges and needn't reach their ends.
Inputs may be any that keep to these rules, and one draw needn't show every extreme that they name: `neg_owner`: the 256 rows of one device name one owner at most 4 times; some device names some owner exactly 4 times.
All inputs are finite; a program needn't handle non-finite values.
Results may differ from the reference program's by a relative error of at most 0.0045.
Values may be sent and summed in bfloat16 or wider, within the bound.
No kernel may reach another device: no remote copies, remote signals or barrier semaphores. Data moves between devices by JAX's collectives and lax.ppermute only.
A program may use at most 64 MiB of HBM per device.

```python
import math
import jax
import jax.numpy as jnp
import numpy as np
from jax import lax

D = 1024
NEG = 32
Q_DEV = 8
P_DEV = 256
CAP = 4
QUERIES = 2048
PASSAGES = 32768
N_DP = 128
N_GROUP = 2


def plant(entries, stream_key, low, high):
    dims = entries.shape
    index_at = [jax.random.randint(jax.random.fold_in(stream_key, axis), (), 0, dims[axis]) for axis in range(len(dims))]
    entries = entries.at[tuple(index_at)].set(low)
    longest = dims.index(max(dims))
    index_at[longest] = (index_at[longest] + 1) % dims[longest]
    return entries.at[tuple(index_at)].set(high)


def strengthened(values, rng, source, target, shards_of, factor):
    owner, partner = [(jnp.arange(values.shape[position]) // (values.shape[position] // shards_of)).reshape([-1 if axis == position else 1 for axis in range(values.ndim)]) for position in (source, target)]
    chosen = jax.random.permutation(rng, shards_of)[partner]
    strong = (owner == chosen) | (owner == (partner + shards_of // 2) % shards_of)
    return jnp.where(strong, factor * values, values)


def level_of(key, extent, shards, least, largest):
    def one(axis_at, blocks):
        draws = jax.random.uniform(jax.random.fold_in(jax.random.fold_in(key, 6), axis_at), (blocks,), jnp.float32, least / len(shards), largest / len(shards))
        return jnp.repeat(jnp.exp(draws), extent[axis_at] // blocks).reshape((-1,) + (1,) * (len(extent) - axis_at - 1))

    factor_of = one(*shards[0])
    for cut in shards[1:]:
        factor_of = factor_of * one(*cut)
    return factor_of


def rank_bounds(number_of, slope):
    weights = [(1 << 20) // math.isqrt(standing ** slope) + 1 for standing in range(1, number_of + 1)]
    width = 1 + sum(weights) // (1 << 30)
    return np.cumsum(np.array([max(1, weight // width) for weight in weights]))


def ranked(stream_key, extent, count, skew):
    table = rank_bounds(count, skew)
    ticket = jax.random.randint(jax.random.fold_in(stream_key, 1), extent, 0, int(table[count - 1]))
    grade = jnp.searchsorted(jnp.asarray(table, jnp.int32), ticket, side="right")
    return jax.random.permutation(jax.random.fold_in(stream_key, 2), count)[grade].astype(jnp.int32)


def assign_block(rng, own, number, rows, number_of, top, most, slope):
    sequence = jax.random.permutation(rng, number_of)
    heavy_load, ordinary = shares(number_of, rows * top, most, slope, True), shares(number_of, rows * top, most, slope, False)
    places = jnp.arange(number_of)

    def named(sizes, offset_by):
        used = int((sizes > 0).sum())
        fixed = max(1, used // 4)
        moved = fixed + (places - fixed + offset_by * (used - fixed)) % max(1, number_of - fixed)
        return jnp.zeros((number_of,), jnp.int32).at[sequence[jnp.where(places < fixed, places, moved)]].set(jnp.asarray(sizes, jnp.int32))

    sizes = jnp.where(number % 4 == 0, named(heavy_load, number // 4), named(ordinary, number - number // 4 - 1))
    mixed = jax.random.permutation(jax.random.fold_in(own, 3), number_of)
    source_of, sink = mixed[0:number_of // 2 * 2:2], mixed[1:number_of // 2 * 2:2]
    room = jnp.minimum(sizes[source_of] - 1, most - sizes[sink]) // 2
    room = jnp.where((source_of == sequence[0]) | (sink == sequence[0]) | (sizes[sink] == 0), 0, jnp.maximum(room, 0))
    moved = jax.random.randint(jax.random.fold_in(own, 4), (number_of // 2,), 0, 1 << 20) % (room + 1)
    sizes = sizes.at[source_of].add(-moved).at[sink].add(moved)
    members = jnp.searchsorted(jnp.cumsum(sizes), jnp.arange(rows * top), side="right").astype(jnp.int32)
    table = members.reshape(top, rows).T
    table = table[jax.random.permutation(jax.random.fold_in(own, 1), rows)]
    offset_by = jax.random.randint(jax.random.fold_in(own, 2), (rows, 1), 0, top)
    return jnp.take_along_axis(table, (jnp.arange(top)[None, :] + offset_by) % top, axis=1)


def shares(amount, total, limit, skew, full):
    weights = [(1 << 20) // math.isqrt(grade ** skew) + 1 for grade in range(1, amount + 1)]
    largest = limit if full else min(limit, max(-(-total // amount), total * weights[0] // sum(weights)))
    least = 1 if total - largest >= amount - 1 else 0
    given, spare = [largest] + [least] * (amount - 1), total - largest - least * (amount - 1)
    while spare > 0:
        free = [i for i in range(1, amount) if given[i] < largest] or [i for i in range(1, amount) if given[i] < limit]
        pool, remaining = sum([weights[i] for i in free]), spare
        for i in free:
            more = min(limit - given[i], max(1, remaining * weights[i] // pool), spare)
            given[i] = given[i] + more
            spare = spare - more
    return np.array(given)


def normal_values(key, extent, scale, most, split=(), held_as=jnp.bfloat16):
    drawn = jax.random.normal(key, extent, jnp.float32) * scale
    if len(split) > 0:
        drawn = level_of(key, extent, split, -0.22, 0.18) * drawn
    return jnp.clip(drawn, min=-most, max=most).astype(held_as)


def noise_with(own_key, dims, deviation, most, cuts, heavy, kind=jnp.bfloat16):
    array = deviation * jax.random.normal(own_key, dims, jnp.float32)
    if cuts:
        array = array * level_of(own_key, dims, cuts, -0.22, 0.18)
    return jnp.clip(strengthened(array, jax.random.fold_in(own_key, 3), *heavy), -most, most).astype(kind)


def setup_inputs(seed: int = 0) -> dict:
    keys = jax.random.split(jax.random.key(seed), 6)
    queries = normal_values(keys[0], (QUERIES, D), 1.0, 6.0, ((0, 256),))
    passage_hidden = noise_with(keys[1], (PASSAGES, D), 1.0, 24.0, ((0, 128),), (0, 1, 128, 5.5))
    out_weight = normal_values(keys[2], (D, D), D ** -0.5, 0.1875)
    neg_owner_keys = jax.random.split(jax.random.fold_in(keys[3], 1), (QUERIES * NEG) // (Q_DEV * NEG))
    neg_owner_turns = jax.random.permutation(jax.random.fold_in(keys[3], 3), (QUERIES * NEG) // (Q_DEV * NEG))
    neg_owner = jax.vmap(lambda own, number: assign_block(jax.random.fold_in(keys[3], 2), own, number, Q_DEV * NEG, N_DP, 1, CAP, 2))(neg_owner_keys, neg_owner_turns).reshape((QUERIES * NEG, 1))
    neg_local = plant(ranked(keys[4], (QUERIES, NEG), P_DEV, 1), jax.random.fold_in(keys[4], 3), 0, P_DEV - 1).astype(jnp.int32)
    return dict(queries=queries, passage_hidden=passage_hidden, out_weight=out_weight, neg_owner=neg_owner, neg_local=neg_local)


def reference(queries, passage_hidden, out_weight, neg_owner, neg_local):
    score_scale = 1.5 / math.sqrt(D)
    embedded = jnp.dot(passage_hidden, out_weight, preferred_element_type=jnp.float32).astype(jnp.bfloat16)
    query_ids = jnp.arange(QUERIES, dtype=jnp.int32)
    pair_rows = N_GROUP * Q_DEV
    pos_ids = (query_ids // pair_rows * P_DEV + query_ids % pair_rows).astype(jnp.int32)
    neg_ids = (neg_owner.reshape(QUERIES, NEG) * P_DEV + neg_local).astype(jnp.int32)
    query_parts = queries.reshape(N_DP, N_GROUP, Q_DEV, D)
    pos_parts = pos_ids.reshape(N_DP, N_GROUP, Q_DEV)
    neg_parts = neg_ids.reshape(N_DP, N_GROUP, Q_DEV, NEG)
    weight_grad = jnp.zeros((D, D), jnp.float32)
    losses = []
    for member in range(N_GROUP):
        query_f32 = query_parts[:, member].reshape(-1, D).astype(jnp.float32)
        pos_sel = pos_parts[:, member].reshape(-1)
        neg_sel = neg_parts[:, member].reshape(-1, NEG)
        pos_keys = embedded[pos_sel].astype(jnp.float32)
        neg_keys = embedded[neg_sel].astype(jnp.float32)
        pos_logit = lax.optimization_barrier(jnp.sum(query_f32 * pos_keys, axis=1)) * score_scale
        neg_logit = jnp.einsum('qd,qjd->qj', query_f32, neg_keys) * score_scale
        logits = jnp.concatenate([pos_logit[:, None], neg_logit], axis=1)
        log_total = jnp.log(lax.optimization_barrier(jnp.sum(jnp.exp(logits), axis=1)))
        losses.append((log_total - pos_logit).reshape(N_DP, Q_DEV))
        soft_prob = jnp.exp(logits - log_total[:, None])
        neg_rows = (soft_prob[:, 1:, None] * score_scale * query_f32[:, None, :]).astype(jnp.bfloat16)
        pos_rows = ((soft_prob[:, 0] - 1.0) * score_scale)[:, None] * query_f32
        embed_grad = jnp.zeros((PASSAGES, D), jnp.float32)
        embed_grad = embed_grad.at[neg_sel.reshape(-1)].add(neg_rows.reshape(-1, D).astype(jnp.float32))
        embed_grad = embed_grad.at[pos_sel].add(pos_rows)
        weight_grad = weight_grad + jnp.dot(passage_hidden.T, embed_grad.astype(jnp.bfloat16), preferred_element_type=jnp.float32)
    query_loss = jnp.stack(losses, axis=1).reshape(QUERIES)
    return (weight_grad, query_loss)
```

```python
import math

import jax
import jax.numpy as jnp
from jax import lax
from jax.sharding import PartitionSpec as P


def transposed_dot(left, right):
    return lax.dot_general(
        left, right, (((0,), (0,)), ((), ())), preferred_element_type=jnp.float32
    )


def local(queries, passage_hidden, out_weight, neg_owner, neg_local):
    dp_count = lax.axis_size("dp")
    group_pos = lax.axis_index("group")
    query_rows, width = queries.shape
    passage_rows = passage_hidden.shape[0]
    neg_count = neg_local.shape[1]
    ref_count = query_rows * neg_count
    capacity = 2 * ref_count // dp_count
    score_scale = 1.5 / math.sqrt(width)
    embedded = jnp.dot(passage_hidden, out_weight, preferred_element_type=jnp.float32).astype(
        jnp.bfloat16
    )
    owners = neg_owner.reshape(ref_count)
    local_ids = neg_local.reshape(ref_count)
    one_hot = (owners[:, None] == jnp.arange(dp_count, dtype=jnp.int32)[None, :]).astype(jnp.int32)
    slot_rank = jnp.sum((jnp.cumsum(one_hot, axis=0) - one_hot) * one_hot, axis=1)
    position = owners * capacity + slot_rank
    requests = (
        jnp.zeros((dp_count * capacity,), jnp.int32)
        .at[position]
        .set(local_ids)
        .reshape(dp_count, capacity)
    )
    id_block = lax.all_to_all(requests, "dp", split_axis=0, concat_axis=0, tiled=True)
    key_block = jnp.take(embedded, id_block, axis=0)
    returned_keys = lax.all_to_all(key_block, "dp", split_axis=0, concat_axis=0, tiled=True)
    neg_keys = jnp.take(
        returned_keys.reshape(dp_count * capacity, width), position, axis=0
    ).reshape(query_rows, neg_count, width)
    own_rows = lax.dynamic_slice_in_dim(embedded, group_pos * query_rows, query_rows, 0)
    pos_logit = (
        jnp.einsum("qd,qd->q", queries, own_rows, preferred_element_type=jnp.float32) * score_scale
    )
    neg_logit = (
        jnp.einsum("qd,qjd->qj", queries, neg_keys, preferred_element_type=jnp.float32)
        * score_scale
    )
    logits = jnp.concatenate([pos_logit[:, None], neg_logit], axis=1)
    log_total = jnp.log(jnp.sum(jnp.exp(logits), axis=1))
    query_loss = log_total - pos_logit
    soft_prob = jnp.exp(logits - log_total[:, None])
    query_f32 = queries.astype(jnp.float32)
    neg_rows = (soft_prob[:, 1:, None] * score_scale * query_f32[:, None, :]).astype(jnp.bfloat16)
    outgoing = (
        jnp.zeros((dp_count * capacity, width), jnp.bfloat16)
        .at[position]
        .set(neg_rows.reshape(ref_count, width))
    )
    returned = lax.all_to_all(
        outgoing.reshape(dp_count, capacity, width), "dp", split_axis=0, concat_axis=0, tiled=True
    )
    embed_grad = jnp.zeros((passage_rows, width), jnp.float32)
    embed_grad = embed_grad.at[id_block.reshape(-1)].add(
        returned.reshape(-1, width).astype(jnp.float32)
    )
    pos_rows = ((soft_prob[:, 0] - 1.0) * score_scale)[:, None] * query_f32
    own_grad = (
        lax.dynamic_slice_in_dim(embed_grad, group_pos * query_rows, query_rows, 0) + pos_rows
    )
    embed_grad = lax.dynamic_update_slice_in_dim(embed_grad, own_grad, group_pos * query_rows, 0)
    grad_bf16 = embed_grad.astype(jnp.bfloat16)
    dw_rows = lax.psum_scatter(
        transposed_dot(passage_hidden, grad_bf16), ("dp", "group"), scatter_dimension=0, tiled=True
    )
    weight_grad = lax.all_gather(dw_rows, "group", axis=0, tiled=True)
    return (weight_grad, query_loss)


def solution(mesh):
    placed = (
        P(("dp", "group"), None),
        P("dp", None),
        P(),
        P(("dp", "group"), None),
        P(("dp", "group"), None),
    )
    return jax.shard_map(
        local,
        mesh=mesh,
        in_specs=placed,
        out_specs=(P("dp", None), P(("dp", "group"))),
        check_vma=False,
    )
```

```python
import math

import jax
import jax.numpy as jnp
from jax import lax
from jax.sharding import PartitionSpec as P


def split_dot(left, right):
    high = left.astype(jnp.bfloat16)
    low = (left - high.astype(jnp.float32)).astype(jnp.bfloat16)
    dims = (((0,), (0,)), ((), ()))
    return lax.dot_general(high, right, dims, preferred_element_type=jnp.float32) + lax.dot_general(
        low, right, dims, preferred_element_type=jnp.float32
    )


def local(queries, passage_hidden, out_weight, neg_owner, neg_local):
    dp_count = lax.axis_size("dp")
    group_pos = lax.axis_index("group")
    query_rows, width = queries.shape
    neg_count = neg_local.shape[1]
    ref_count = query_rows * neg_count
    capacity = 2 * ref_count // dp_count
    out_rows = out_weight.shape[0] // dp_count
    score_scale = 1.5 / math.sqrt(width)
    all_queries = lax.all_gather(queries, ("dp", "group"), axis=0, tiled=True)
    owners = neg_owner.reshape(ref_count)
    local_ids = neg_local.reshape(ref_count)
    one_hot = (owners[:, None] == jnp.arange(dp_count, dtype=jnp.int32)[None, :]).astype(jnp.int32)
    slot_rank = jnp.sum((jnp.cumsum(one_hot, axis=0) - one_hot) * one_hot, axis=1)
    position = owners * capacity + slot_rank
    requests = (
        jnp.zeros((dp_count * capacity,), jnp.int32)
        .at[position]
        .set(local_ids)
        .reshape(dp_count, capacity)
    )
    id_block = lax.all_to_all(requests, "dp", split_axis=0, concat_axis=0, tiled=True)
    hidden_block = jnp.take(passage_hidden, id_block, axis=0)
    returned_hidden = lax.all_to_all(hidden_block, "dp", split_axis=0, concat_axis=0, tiled=True)
    neg_hidden = jnp.take(returned_hidden.reshape(dp_count * capacity, width), position, axis=0)
    pos_hidden = lax.dynamic_slice_in_dim(passage_hidden, group_pos * query_rows, query_rows, 0)
    neg_keys = jnp.dot(neg_hidden, out_weight, preferred_element_type=jnp.float32).astype(
        jnp.bfloat16
    ).reshape(query_rows, neg_count, width)
    pos_keys = jnp.dot(pos_hidden, out_weight, preferred_element_type=jnp.float32).astype(
        jnp.bfloat16
    )
    pos_logit = (
        jnp.einsum("qd,qd->q", queries, pos_keys, preferred_element_type=jnp.float32) * score_scale
    )
    neg_logit = (
        jnp.einsum("qd,qjd->qj", queries, neg_keys, preferred_element_type=jnp.float32)
        * score_scale
    )
    logits = jnp.concatenate([pos_logit[:, None], neg_logit], axis=1)
    log_total = jnp.log(jnp.sum(jnp.exp(logits), axis=1))
    query_loss = log_total - pos_logit
    soft_prob = jnp.exp(logits - log_total[:, None])
    neg_coef = soft_prob[:, 1:] * score_scale
    pos_coef = (soft_prob[:, 0] - 1.0) * score_scale
    mixed = jnp.sum(
        neg_coef[:, :, None] * neg_hidden.reshape(query_rows, neg_count, width).astype(jnp.float32),
        axis=1,
    ) + pos_coef[:, None] * pos_hidden.astype(jnp.float32)
    mixed_cols = mixed.reshape(query_rows, dp_count, out_rows).transpose(1, 0, 2)
    mixed_cols = lax.all_to_all(mixed_cols, "dp", split_axis=0, concat_axis=0, tiled=True)
    mixed_cols = lax.all_gather(mixed_cols, "group", axis=0)
    mixed_cols = mixed_cols.transpose(1, 0, 2, 3).reshape(-1, out_rows)
    weight_grad = split_dot(mixed_cols, all_queries)
    return (weight_grad, query_loss)


def solution(mesh):
    placed = (
        P(("dp", "group"), None),
        P("dp", None),
        P(),
        P(("dp", "group"), None),
        P(("dp", "group"), None),
    )
    return jax.shard_map(
        local,
        mesh=mesh,
        in_specs=placed,
        out_specs=(P("dp", None), P(("dp", "group"))),
        check_vma=False,
    )
```

```python
import math

import jax
import jax.numpy as jnp
from jax import lax
from jax.sharding import PartitionSpec as P


def split_dot(left, right):
    high = left.astype(jnp.bfloat16)
    low = (left - high.astype(jnp.float32)).astype(jnp.bfloat16)
    dims = (((0,), (0,)), ((), ()))
    return lax.dot_general(high, right, dims, preferred_element_type=jnp.float32) + lax.dot_general(
        low, right, dims, preferred_element_type=jnp.float32
    )


def local(queries, passage_hidden, out_weight, neg_owner, neg_local):
    dp_count = lax.axis_size("dp")
    group_pos = lax.axis_index("group")
    query_rows, width = queries.shape
    neg_count = neg_local.shape[1]
    ref_count = query_rows * neg_count
    capacity = 2 * ref_count // dp_count
    out_rows = out_weight.shape[0] // dp_count
    score_scale = 1.5 / math.sqrt(width)
    col_half = width // 2
    pair_queries = lax.all_gather(queries, "group", axis=0, tiled=True)
    own_half = lax.dynamic_slice_in_dim(pair_queries, group_pos * col_half, col_half, 1)
    all_queries = lax.all_gather(own_half, "dp", axis=0, tiled=True)
    owners = neg_owner.reshape(ref_count)
    local_ids = neg_local.reshape(ref_count)
    one_hot = (owners[:, None] == jnp.arange(dp_count, dtype=jnp.int32)[None, :]).astype(jnp.int32)
    slot_rank = jnp.sum((jnp.cumsum(one_hot, axis=0) - one_hot) * one_hot, axis=1)
    position = owners * capacity + slot_rank
    requests = (
        jnp.zeros((dp_count * capacity,), jnp.int32)
        .at[position]
        .set(local_ids)
        .reshape(dp_count, capacity)
    )
    id_block = lax.all_to_all(requests, "dp", split_axis=0, concat_axis=0, tiled=True)
    hidden_block = jnp.take(passage_hidden, id_block, axis=0)
    returned_hidden = lax.all_to_all(hidden_block, "dp", split_axis=0, concat_axis=0, tiled=True)
    neg_hidden = jnp.take(returned_hidden.reshape(dp_count * capacity, width), position, axis=0)
    pos_hidden = lax.dynamic_slice_in_dim(passage_hidden, group_pos * query_rows, query_rows, 0)
    neg_keys = jnp.dot(neg_hidden, out_weight, preferred_element_type=jnp.float32).astype(
        jnp.bfloat16
    ).reshape(query_rows, neg_count, width)
    pos_keys = jnp.dot(pos_hidden, out_weight, preferred_element_type=jnp.float32).astype(
        jnp.bfloat16
    )
    pos_logit = (
        jnp.einsum("qd,qd->q", queries, pos_keys, preferred_element_type=jnp.float32) * score_scale
    )
    neg_logit = (
        jnp.einsum("qd,qjd->qj", queries, neg_keys, preferred_element_type=jnp.float32)
        * score_scale
    )
    logits = jnp.concatenate([pos_logit[:, None], neg_logit], axis=1)
    log_total = jnp.log(jnp.sum(jnp.exp(logits), axis=1))
    query_loss = log_total - pos_logit
    soft_prob = jnp.exp(logits - log_total[:, None])
    neg_coef = soft_prob[:, 1:] * score_scale
    pos_coef = (soft_prob[:, 0] - 1.0) * score_scale
    mixed = jnp.sum(
        neg_coef[:, :, None] * neg_hidden.reshape(query_rows, neg_count, width).astype(jnp.float32),
        axis=1,
    ) + pos_coef[:, None] * pos_hidden.astype(jnp.float32)
    mixed_cols = mixed.reshape(query_rows, dp_count, out_rows).transpose(1, 0, 2)
    mixed_cols = lax.all_to_all(mixed_cols, "dp", split_axis=0, concat_axis=0, tiled=True)
    mixed_cols = lax.all_gather(mixed_cols, "group", axis=0)
    mixed_cols = mixed_cols.transpose(1, 0, 2, 3).reshape(-1, out_rows)
    weight_half = split_dot(mixed_cols, all_queries)
    weight_grad = lax.all_gather(weight_half, "group", axis=1, tiled=True)
    return (weight_grad, query_loss)


def solution(mesh):
    placed = (
        P(("dp", "group"), None),
        P("dp", None),
        P(),
        P(("dp", "group"), None),
        P(("dp", "group"), None),
    )
    return jax.shard_map(
        local,
        mesh=mesh,
        in_specs=placed,
        out_specs=(P("dp", None), P(("dp", "group"))),
        check_vma=False,
    )
```

```python
import math

import jax
import jax.numpy as jnp
from jax import lax
from jax.sharding import PartitionSpec as P


def split_dot(left, right):
    high = left.astype(jnp.bfloat16)
    low = (left - high.astype(jnp.float32)).astype(jnp.bfloat16)
    dims = (((0,), (0,)), ((), ()))
    return lax.dot_general(high, right, dims, preferred_element_type=jnp.float32) + lax.dot_general(
        low, right, dims, preferred_element_type=jnp.float32
    )


def local(queries, passage_hidden, out_weight, neg_owner, neg_local):
    dp_count = lax.axis_size("dp")
    group_pos = lax.axis_index("group")
    query_rows, width = queries.shape
    neg_count = neg_local.shape[1]
    ref_count = query_rows * neg_count
    capacity = 2 * ref_count // dp_count
    out_rows = out_weight.shape[0] // dp_count
    score_scale = 1.5 / math.sqrt(width)
    owners = neg_owner.reshape(ref_count)
    local_ids = neg_local.reshape(ref_count)
    one_hot = (owners[:, None] == jnp.arange(dp_count, dtype=jnp.int32)[None, :]).astype(jnp.int32)
    slot_rank = jnp.sum((jnp.cumsum(one_hot, axis=0) - one_hot) * one_hot, axis=1)
    position = owners * capacity + slot_rank
    requests = (
        jnp.zeros((dp_count * capacity,), jnp.int32)
        .at[position]
        .set(local_ids)
        .reshape(dp_count, capacity)
    )
    id_block = lax.all_to_all(requests, "dp", split_axis=0, concat_axis=0, tiled=True)
    hidden_block = jnp.take(passage_hidden, id_block, axis=0, mode="clip")
    returned_hidden = lax.all_to_all(hidden_block, "dp", split_axis=0, concat_axis=0, tiled=True)
    neg_hidden = jnp.take(
        returned_hidden.reshape(dp_count * capacity, width), position, axis=0, mode="clip"
    )
    pos_hidden = lax.dynamic_slice_in_dim(passage_hidden, group_pos * query_rows, query_rows, 0)
    neg_keys = jnp.dot(neg_hidden, out_weight, preferred_element_type=jnp.float32).astype(
        jnp.bfloat16
    ).reshape(query_rows, neg_count, width)
    pos_keys = jnp.dot(pos_hidden, out_weight, preferred_element_type=jnp.float32).astype(
        jnp.bfloat16
    )
    pos_logit = (
        jnp.einsum("qd,qd->q", queries, pos_keys, preferred_element_type=jnp.float32) * score_scale
    )
    neg_logit = (
        jnp.einsum("qd,qjd->qj", queries, neg_keys, preferred_element_type=jnp.float32)
        * score_scale
    )
    logits = jnp.concatenate([pos_logit[:, None], neg_logit], axis=1)
    log_total = jnp.log(jnp.sum(jnp.exp(logits), axis=1))
    query_loss = log_total - pos_logit
    soft_prob = jnp.exp(logits - log_total[:, None])
    neg_coef = soft_prob[:, 1:] * score_scale
    pos_coef = (soft_prob[:, 0] - 1.0) * score_scale
    mixed = jnp.sum(
        neg_coef[:, :, None] * neg_hidden.reshape(query_rows, neg_count, width).astype(jnp.float32),
        axis=1,
    ) + pos_coef[:, None] * pos_hidden.astype(jnp.float32)
    col_half = width // 2
    chip_mixed = lax.all_gather(mixed, "group", axis=0, tiled=True)
    chip_queries = lax.all_gather(queries, "group", axis=0, tiled=True)
    half_queries = lax.dynamic_slice_in_dim(chip_queries, group_pos * col_half, col_half, 1)
    partial = split_dot(chip_mixed, half_queries).reshape(dp_count, out_rows, col_half)
    partial = lax.all_to_all(partial, "dp", split_axis=0, concat_axis=0, tiled=True)
    weight_half = jnp.sum(partial, axis=0)
    weight_grad = lax.all_gather(weight_half, "group", axis=1, tiled=True)
    return (weight_grad, query_loss)


def solution(mesh):
    placed = (
        P(("dp", "group"), None),
        P("dp", None),
        P(),
        P(("dp", "group"), None),
        P(("dp", "group"), None),
    )
    return jax.shard_map(
        local,
        mesh=mesh,
        in_specs=placed,
        out_specs=(P("dp", None), P(("dp", "group"))),
        check_vma=False,
    )
```

```python
import math

import jax
import jax.numpy as jnp
from jax import lax
from jax.sharding import PartitionSpec as P


def split_dot(left, right):
    high = left.astype(jnp.bfloat16)
    low = (left - high.astype(jnp.float32)).astype(jnp.bfloat16)
    dims = (((0,), (0,)), ((), ()))
    return lax.dot_general(high, right, dims, preferred_element_type=jnp.float32) + lax.dot_general(
        low, right, dims, preferred_element_type=jnp.float32
    )


def local(queries, passage_hidden, out_weight, neg_owner, neg_local):
    dp_count = lax.axis_size("dp")
    group_pos = lax.axis_index("group")
    query_rows, width = queries.shape
    neg_count = neg_local.shape[1]
    ref_count = query_rows * neg_count
    capacity = 2 * ref_count // dp_count
    out_rows = out_weight.shape[0] // dp_count
    score_scale = 1.5 / math.sqrt(width)
    owners = neg_owner.reshape(ref_count)
    local_ids = neg_local.reshape(ref_count)
    one_hot = (owners[:, None] == jnp.arange(dp_count, dtype=jnp.int32)[None, :]).astype(jnp.int32)
    slot_rank = jnp.sum((jnp.cumsum(one_hot, axis=0) - one_hot) * one_hot, axis=1)
    position = owners * capacity + slot_rank
    requests = (
        jnp.zeros((dp_count * capacity,), jnp.int32)
        .at[position]
        .set(local_ids)
        .reshape(dp_count, capacity)
    )
    id_block = lax.all_to_all(requests, "dp", split_axis=0, concat_axis=0, tiled=True)
    hidden_block = jnp.take(passage_hidden, id_block, axis=0, mode="clip")
    returned_hidden = lax.all_to_all(hidden_block, "dp", split_axis=0, concat_axis=0, tiled=True)
    neg_hidden = jnp.take(
        returned_hidden.reshape(dp_count * capacity, width), position, axis=0, mode="clip"
    )
    pos_hidden = lax.dynamic_slice_in_dim(passage_hidden, group_pos * query_rows, query_rows, 0)
    neg_keys = jnp.dot(neg_hidden, out_weight, preferred_element_type=jnp.float32).astype(
        jnp.bfloat16
    ).reshape(query_rows, neg_count, width)
    pos_keys = jnp.dot(pos_hidden, out_weight, preferred_element_type=jnp.float32).astype(
        jnp.bfloat16
    )
    pos_logit = (
        jnp.einsum("qd,qd->q", queries, pos_keys, preferred_element_type=jnp.float32) * score_scale
    )
    neg_logit = (
        jnp.einsum("qd,qjd->qj", queries, neg_keys, preferred_element_type=jnp.float32)
        * score_scale
    )
    logits = jnp.concatenate([pos_logit[:, None], neg_logit], axis=1)
    log_total = jnp.log(jnp.sum(jnp.exp(logits), axis=1))
    query_loss = log_total - pos_logit
    soft_prob = jnp.exp(logits - log_total[:, None])
    neg_coef = soft_prob[:, 1:] * score_scale
    pos_coef = (soft_prob[:, 0] - 1.0) * score_scale
    mixed = jnp.sum(
        neg_coef[:, :, None] * neg_hidden.reshape(query_rows, neg_count, width).astype(jnp.float32),
        axis=1,
    ) + pos_coef[:, None] * pos_hidden.astype(jnp.float32)
    col_half = width // 2
    chip_mixed = lax.all_gather(mixed, "group", axis=0, tiled=True)
    chip_queries = lax.all_gather(queries, "group", axis=0, tiled=True)
    half_queries = lax.dynamic_slice_in_dim(chip_queries, group_pos * col_half, col_half, 1)
    partial = split_dot(chip_mixed, half_queries).astype(jnp.bfloat16)
    partial = partial.reshape(dp_count, out_rows, col_half)
    partial = lax.all_to_all(partial, "dp", split_axis=0, concat_axis=0, tiled=True)
    weight_half = jnp.sum(partial.astype(jnp.float32), axis=0)
    weight_grad = lax.all_gather(weight_half, "group", axis=1, tiled=True)
    return (weight_grad, query_loss)


def solution(mesh):
    placed = (
        P(("dp", "group"), None),
        P("dp", None),
        P(),
        P(("dp", "group"), None),
        P(("dp", "group"), None),
    )
    return jax.shard_map(
        local,
        mesh=mesh,
        in_specs=placed,
        out_specs=(P("dp", None), P(("dp", "group"))),
        check_vma=False,
    )
```

```python
import math

import jax
import jax.numpy as jnp
from jax import lax
from jax.sharding import PartitionSpec as P


def split_dot(left, right):
    high = left.astype(jnp.bfloat16)
    low = (left - high.astype(jnp.float32)).astype(jnp.bfloat16)
    dims = (((0,), (0,)), ((), ()))
    return lax.dot_general(high, right, dims, preferred_element_type=jnp.float32) + lax.dot_general(
        low, right, dims, preferred_element_type=jnp.float32
    )


def local(queries, passage_hidden, out_weight, neg_owner, neg_local):
    dp_count = lax.axis_size("dp")
    group_pos = lax.axis_index("group")
    query_rows, width = queries.shape
    passage_rows = passage_hidden.shape[0]
    neg_count = neg_local.shape[1]
    ref_count = query_rows * neg_count
    capacity = 2 * ref_count // dp_count
    out_rows = out_weight.shape[0] // dp_count
    score_scale = 1.5 / math.sqrt(width)
    owners = neg_owner.reshape(ref_count)
    local_ids = neg_local.reshape(ref_count)
    one_hot = (owners[:, None] == jnp.arange(dp_count, dtype=jnp.int32)[None, :]).astype(jnp.int32)
    slot_rank = jnp.sum((jnp.cumsum(one_hot, axis=0) - one_hot) * one_hot, axis=1)
    position = owners * capacity + slot_rank
    requests = (
        jnp.zeros((dp_count * capacity,), jnp.int32)
        .at[position]
        .set(local_ids)
        .reshape(dp_count, capacity)
    )
    id_block = lax.all_to_all(requests, "dp", split_axis=0, concat_axis=0, tiled=True)
    pick_send = (
        id_block[:, :, None] == jnp.arange(passage_rows, dtype=jnp.int32)[None, None, :]
    ).astype(jnp.bfloat16)
    hidden_block = jnp.einsum(
        "kcp,pd->kcd", pick_send, passage_hidden, preferred_element_type=jnp.float32
    ).astype(jnp.bfloat16)
    returned_hidden = lax.all_to_all(hidden_block, "dp", split_axis=0, concat_axis=0, tiled=True)
    pick_back = (
        position[:, None, None]
        == (jnp.arange(dp_count * capacity, dtype=jnp.int32).reshape(1, dp_count, capacity))
    ).astype(jnp.bfloat16)
    neg_hidden = jnp.einsum(
        "rkc,kcd->rd", pick_back, returned_hidden, preferred_element_type=jnp.float32
    ).astype(jnp.bfloat16)
    pos_hidden = lax.dynamic_slice_in_dim(passage_hidden, group_pos * query_rows, query_rows, 0)
    neg_keys = jnp.dot(neg_hidden, out_weight, preferred_element_type=jnp.float32).astype(
        jnp.bfloat16
    ).reshape(query_rows, neg_count, width)
    pos_keys = jnp.dot(pos_hidden, out_weight, preferred_element_type=jnp.float32).astype(
        jnp.bfloat16
    )
    pos_logit = (
        jnp.einsum("qd,qd->q", queries, pos_keys, preferred_element_type=jnp.float32) * score_scale
    )
    neg_logit = (
        jnp.einsum("qd,qjd->qj", queries, neg_keys, preferred_element_type=jnp.float32)
        * score_scale
    )
    logits = jnp.concatenate([pos_logit[:, None], neg_logit], axis=1)
    log_total = jnp.log(jnp.sum(jnp.exp(logits), axis=1))
    query_loss = log_total - pos_logit
    soft_prob = jnp.exp(logits - log_total[:, None])
    neg_coef = soft_prob[:, 1:] * score_scale
    pos_coef = (soft_prob[:, 0] - 1.0) * score_scale
    mixed = jnp.sum(
        neg_coef[:, :, None] * neg_hidden.reshape(query_rows, neg_count, width).astype(jnp.float32),
        axis=1,
    ) + pos_coef[:, None] * pos_hidden.astype(jnp.float32)
    col_half = width // 2
    chip_mixed = lax.all_gather(mixed, "group", axis=0, tiled=True)
    chip_queries = lax.all_gather(queries, "group", axis=0, tiled=True)
    half_queries = lax.dynamic_slice_in_dim(chip_queries, group_pos * col_half, col_half, 1)
    partial = split_dot(chip_mixed, half_queries).astype(jnp.bfloat16)
    partial = partial.reshape(dp_count, out_rows, col_half)
    partial = lax.all_to_all(partial, "dp", split_axis=0, concat_axis=0, tiled=True)
    weight_half = jnp.sum(partial.astype(jnp.float32), axis=0)
    weight_grad = lax.all_gather(weight_half, "group", axis=1, tiled=True)
    return (weight_grad, query_loss)


def solution(mesh):
    placed = (
        P(("dp", "group"), None),
        P("dp", None),
        P(),
        P(("dp", "group"), None),
        P(("dp", "group"), None),
    )
    return jax.shard_map(
        local,
        mesh=mesh,
        in_specs=placed,
        out_specs=(P("dp", None), P(("dp", "group"))),
        check_vma=False,
    )
```

```python
import math

import jax
import jax.numpy as jnp
from jax import lax
from jax.sharding import PartitionSpec as P


def split_dot(left, right):
    high = left.astype(jnp.bfloat16)
    low = (left - high.astype(jnp.float32)).astype(jnp.bfloat16)
    dims = (((0,), (0,)), ((), ()))
    return lax.dot_general(high, right, dims, preferred_element_type=jnp.float32) + lax.dot_general(
        low, right, dims, preferred_element_type=jnp.float32
    )


def local(queries, passage_hidden, out_weight, neg_owner, neg_local):
    dp_count = lax.axis_size("dp")
    group_pos = lax.axis_index("group")
    query_rows, width = queries.shape
    passage_rows = passage_hidden.shape[0]
    neg_count = neg_local.shape[1]
    ref_count = query_rows * neg_count
    capacity = 2 * ref_count // dp_count
    out_rows = out_weight.shape[0] // dp_count
    score_scale = 1.5 / math.sqrt(width)
    owners = neg_owner.reshape(ref_count)
    local_ids = neg_local.reshape(ref_count)
    ref_index = jnp.arange(ref_count, dtype=jnp.int32)
    same_owner = (owners[:, None] == owners[None, :]) & (ref_index[:, None] > ref_index[None, :])
    slot_rank = jnp.sum(same_owner.astype(jnp.int32), axis=1)
    position = owners * capacity + slot_rank
    place = (
        position[:, None] == jnp.arange(dp_count * capacity, dtype=jnp.int32)[None, :]
    ).astype(jnp.bfloat16)
    requests = (
        jnp.dot(local_ids.astype(jnp.bfloat16), place, preferred_element_type=jnp.float32)
        .astype(jnp.int32)
        .reshape(dp_count, capacity)
    )
    id_block = lax.all_to_all(requests, "dp", split_axis=0, concat_axis=0, tiled=True)
    pick_send = (
        id_block[:, :, None] == jnp.arange(passage_rows, dtype=jnp.int32)[None, None, :]
    ).astype(jnp.bfloat16)
    hidden_block = jnp.einsum(
        "kcp,pd->kcd", pick_send, passage_hidden, preferred_element_type=jnp.float32
    ).astype(jnp.bfloat16)
    returned_hidden = lax.all_to_all(hidden_block, "dp", split_axis=0, concat_axis=0, tiled=True)
    pick_back = (
        position[:, None, None]
        == (jnp.arange(dp_count * capacity, dtype=jnp.int32).reshape(1, dp_count, capacity))
    ).astype(jnp.bfloat16)
    neg_hidden = jnp.einsum(
        "rkc,kcd->rd", pick_back, returned_hidden, preferred_element_type=jnp.float32
    ).astype(jnp.bfloat16)
    pos_hidden = lax.dynamic_slice_in_dim(passage_hidden, group_pos * query_rows, query_rows, 0)
    neg_keys = jnp.dot(neg_hidden, out_weight, preferred_element_type=jnp.float32).astype(
        jnp.bfloat16
    ).reshape(query_rows, neg_count, width)
    pos_keys = jnp.dot(pos_hidden, out_weight, preferred_element_type=jnp.float32).astype(
        jnp.bfloat16
    )
    pos_logit = (
        jnp.einsum("qd,qd->q", queries, pos_keys, preferred_element_type=jnp.float32) * score_scale
    )
    neg_logit = (
        jnp.einsum("qd,qjd->qj", queries, neg_keys, preferred_element_type=jnp.float32)
        * score_scale
    )
    logits = jnp.concatenate([pos_logit[:, None], neg_logit], axis=1)
    log_total = jnp.log(jnp.sum(jnp.exp(logits), axis=1))
    query_loss = log_total - pos_logit
    soft_prob = jnp.exp(logits - log_total[:, None])
    neg_coef = soft_prob[:, 1:] * score_scale
    pos_coef = (soft_prob[:, 0] - 1.0) * score_scale
    mixed = jnp.sum(
        neg_coef[:, :, None] * neg_hidden.reshape(query_rows, neg_count, width).astype(jnp.float32),
        axis=1,
    ) + pos_coef[:, None] * pos_hidden.astype(jnp.float32)
    col_half = width // 2
    chip_mixed = lax.all_gather(mixed, "group", axis=0, tiled=True)
    chip_queries = lax.all_gather(queries, "group", axis=0, tiled=True)
    half_queries = lax.dynamic_slice_in_dim(chip_queries, group_pos * col_half, col_half, 1)
    partial = split_dot(chip_mixed, half_queries).astype(jnp.bfloat16)
    partial = partial.reshape(dp_count, out_rows, col_half)
    partial = lax.all_to_all(partial, "dp", split_axis=0, concat_axis=0, tiled=True)
    weight_half = jnp.sum(partial.astype(jnp.float32), axis=0)
    weight_grad = lax.all_gather(weight_half, "group", axis=1, tiled=True)
    return (weight_grad, query_loss)


def solution(mesh):
    placed = (
        P(("dp", "group"), None),
        P("dp", None),
        P(),
        P(("dp", "group"), None),
        P(("dp", "group"), None),
    )
    return jax.shard_map(
        local,
        mesh=mesh,
        in_specs=placed,
        out_specs=(P("dp", None), P(("dp", "group"))),
        check_vma=False,
    )
```

```python
import math

import jax
import jax.numpy as jnp
from jax import lax
from jax.sharding import PartitionSpec as P


def split_dot(left, right):
    high = left.astype(jnp.bfloat16)
    low = (left - high.astype(jnp.float32)).astype(jnp.bfloat16)
    dims = (((0,), (0,)), ((), ()))
    return lax.dot_general(high, right, dims, preferred_element_type=jnp.float32) + lax.dot_general(
        low, right, dims, preferred_element_type=jnp.float32
    )


def local(queries, passage_hidden, out_weight, neg_owner, neg_local):
    dp_count = lax.axis_size("dp")
    group_pos = lax.axis_index("group")
    query_rows, width = queries.shape
    passage_rows = passage_hidden.shape[0]
    neg_count = neg_local.shape[1]
    ref_count = query_rows * neg_count
    capacity = 2 * ref_count // dp_count
    out_rows = out_weight.shape[0] // dp_count
    score_scale = 1.5 / math.sqrt(width)
    owners = neg_owner.reshape(ref_count)
    local_ids = neg_local.reshape(ref_count)
    ref_index = jnp.arange(ref_count, dtype=jnp.int32)
    same_owner = (owners[:, None] == owners[None, :]) & (ref_index[:, None] > ref_index[None, :])
    slot_rank = jnp.sum(same_owner.astype(jnp.int32), axis=1)
    position = owners * capacity + slot_rank
    place = (
        position[:, None] == jnp.arange(dp_count * capacity, dtype=jnp.int32)[None, :]
    ).astype(jnp.bfloat16)
    requests = (
        jnp.dot(local_ids.astype(jnp.bfloat16), place, preferred_element_type=jnp.float32)
        .astype(jnp.int32)
        .reshape(dp_count, capacity)
    )
    id_block = lax.all_to_all(requests, "dp", split_axis=0, concat_axis=0, tiled=True)
    pick_send = (
        id_block[:, :, None] == jnp.arange(passage_rows, dtype=jnp.int32)[None, None, :]
    ).astype(jnp.bfloat16)
    hidden_block = jnp.einsum(
        "kcp,pd->kcd", pick_send, passage_hidden, preferred_element_type=jnp.float32
    ).astype(jnp.bfloat16)
    returned_hidden = lax.all_to_all(hidden_block, "dp", split_axis=0, concat_axis=0, tiled=True)
    pick_back = (
        position[:, None, None]
        == (jnp.arange(dp_count * capacity, dtype=jnp.int32).reshape(1, dp_count, capacity))
    ).astype(jnp.bfloat16)
    neg_hidden = jnp.einsum(
        "rkc,kcd->rd", pick_back, returned_hidden, preferred_element_type=jnp.float32
    ).astype(jnp.bfloat16)
    pos_hidden = lax.dynamic_slice_in_dim(passage_hidden, group_pos * query_rows, query_rows, 0)
    neg_keys = jnp.dot(neg_hidden, out_weight, preferred_element_type=jnp.float32).astype(
        jnp.bfloat16
    ).reshape(query_rows, neg_count, width)
    pos_keys = jnp.dot(pos_hidden, out_weight, preferred_element_type=jnp.float32).astype(
        jnp.bfloat16
    )
    pos_logit = (
        jnp.einsum("qd,qd->q", queries, pos_keys, preferred_element_type=jnp.float32) * score_scale
    )
    neg_logit = (
        jnp.einsum("qd,qjd->qj", queries, neg_keys, preferred_element_type=jnp.float32)
        * score_scale
    )
    logits = jnp.concatenate([pos_logit[:, None], neg_logit], axis=1)
    log_total = jnp.log(jnp.sum(jnp.exp(logits), axis=1))
    query_loss = log_total - pos_logit
    soft_prob = jnp.exp(logits - log_total[:, None])
    neg_coef = soft_prob[:, 1:] * score_scale
    pos_coef = (soft_prob[:, 0] - 1.0) * score_scale
    mixed = jnp.sum(
        neg_coef[:, :, None] * neg_hidden.reshape(query_rows, neg_count, width).astype(jnp.float32),
        axis=1,
    ) + pos_coef[:, None] * pos_hidden.astype(jnp.float32)
    col_half = width // 2
    chip_mixed = lax.all_gather(mixed, "group", axis=0, tiled=True)
    chip_queries = lax.all_gather(queries, "group", axis=0, tiled=True)
    half_queries = lax.dynamic_slice_in_dim(chip_queries, group_pos * col_half, col_half, 1)
    partial = split_dot(chip_mixed, half_queries).astype(jnp.bfloat16)
    partial = partial.reshape(dp_count, 2 * out_rows, col_half // 2)
    partial = lax.all_to_all(partial, "dp", split_axis=0, concat_axis=0, tiled=True)
    weight_half = jnp.sum(partial.astype(jnp.float32), axis=0).reshape(out_rows, col_half)
    weight_grad = lax.all_gather(weight_half, "group", axis=1, tiled=True)
    return (weight_grad, query_loss)


def solution(mesh):
    placed = (
        P(("dp", "group"), None),
        P("dp", None),
        P(),
        P(("dp", "group"), None),
        P(("dp", "group"), None),
    )
    return jax.shard_map(
        local,
        mesh=mesh,
        in_specs=placed,
        out_specs=(P("dp", None), P(("dp", "group"))),
        check_vma=False,
    )
```

```python
import math

import jax
import jax.numpy as jnp
from jax import lax
from jax.sharding import PartitionSpec as P


def split_dot(left, right):
    high = left.astype(jnp.bfloat16)
    low = (left - high.astype(jnp.float32)).astype(jnp.bfloat16)
    dims = (((0,), (0,)), ((), ()))
    return lax.dot_general(high, right, dims, preferred_element_type=jnp.float32) + lax.dot_general(
        low, right, dims, preferred_element_type=jnp.float32
    )


def local(queries, passage_hidden, out_weight, neg_owner, neg_local):
    dp_count = lax.axis_size("dp")
    group_pos = lax.axis_index("group")
    query_rows, width = queries.shape
    passage_rows = passage_hidden.shape[0]
    neg_count = neg_local.shape[1]
    ref_count = query_rows * neg_count
    capacity = 2 * ref_count // dp_count
    out_rows = out_weight.shape[0] // dp_count
    score_scale = 1.5 / math.sqrt(width)
    owners = neg_owner.reshape(ref_count)
    local_ids = neg_local.reshape(ref_count)
    ref_index = jnp.arange(ref_count, dtype=jnp.int32)
    same_owner = (owners[:, None] == owners[None, :]) & (ref_index[:, None] > ref_index[None, :])
    slot_rank = jnp.sum(same_owner.astype(jnp.int32), axis=1)
    position = owners * capacity + slot_rank
    slots = jnp.arange(dp_count * capacity, dtype=jnp.int32)
    requests = jnp.sum(
        jnp.where(position[:, None] == slots[None, :], local_ids[:, None], 0), axis=0
    ).reshape(dp_count, capacity)
    id_block = lax.all_to_all(requests, "dp", split_axis=0, concat_axis=0, tiled=True)
    pick_send = (
        id_block[:, :, None] == jnp.arange(passage_rows, dtype=jnp.int32)[None, None, :]
    ).astype(jnp.bfloat16)
    hidden_block = jnp.einsum(
        "kcp,pd->kcd", pick_send, passage_hidden, preferred_element_type=jnp.float32
    ).astype(jnp.bfloat16)
    returned_hidden = lax.all_to_all(hidden_block, "dp", split_axis=0, concat_axis=0, tiled=True)
    pick_back = (
        position[:, None, None]
        == (jnp.arange(dp_count * capacity, dtype=jnp.int32).reshape(1, dp_count, capacity))
    ).astype(jnp.bfloat16)
    neg_hidden = jnp.einsum(
        "rkc,kcd->rd", pick_back, returned_hidden, preferred_element_type=jnp.float32
    ).astype(jnp.bfloat16)
    pos_hidden = lax.dynamic_slice_in_dim(passage_hidden, group_pos * query_rows, query_rows, 0)
    neg_keys = jnp.dot(neg_hidden, out_weight, preferred_element_type=jnp.float32).astype(
        jnp.bfloat16
    ).reshape(query_rows, neg_count, width)
    pos_keys = jnp.dot(pos_hidden, out_weight, preferred_element_type=jnp.float32).astype(
        jnp.bfloat16
    )
    pos_logit = (
        jnp.einsum("qd,qd->q", queries, pos_keys, preferred_element_type=jnp.float32) * score_scale
    )
    neg_logit = (
        jnp.einsum("qd,qjd->qj", queries, neg_keys, preferred_element_type=jnp.float32)
        * score_scale
    )
    logits = jnp.concatenate([pos_logit[:, None], neg_logit], axis=1)
    log_total = jnp.log(jnp.sum(jnp.exp(logits), axis=1))
    query_loss = log_total - pos_logit
    soft_prob = jnp.exp(logits - log_total[:, None])
    neg_coef = soft_prob[:, 1:] * score_scale
    pos_coef = (soft_prob[:, 0] - 1.0) * score_scale
    mixed = jnp.sum(
        neg_coef[:, :, None] * neg_hidden.reshape(query_rows, neg_count, width).astype(jnp.float32),
        axis=1,
    ) + pos_coef[:, None] * pos_hidden.astype(jnp.float32)
    col_half = width // 2
    swap = [(0, 1), (1, 0)]
    other_mixed = lax.ppermute(mixed, "group", swap)
    other_queries = lax.ppermute(queries, "group", swap)
    own_cols = lax.dynamic_slice_in_dim(queries, group_pos * col_half, col_half, 1)
    other_cols = lax.dynamic_slice_in_dim(other_queries, group_pos * col_half, col_half, 1)
    partial = split_dot(mixed, own_cols) + split_dot(other_mixed, other_cols)
    partial = partial.astype(jnp.bfloat16).reshape(dp_count, out_rows, col_half)
    partial = lax.all_to_all(partial, "dp", split_axis=0, concat_axis=0, tiled=True)
    weight_half = jnp.sum(partial.astype(jnp.float32), axis=0)
    other_half = lax.ppermute(weight_half, "group", swap)
    weight_grad = jnp.where(
        group_pos == 0,
        jnp.concatenate([weight_half, other_half], axis=1),
        jnp.concatenate([other_half, weight_half], axis=1),
    )
    return (weight_grad, query_loss)


def solution(mesh):
    placed = (
        P(("dp", "group"), None),
        P("dp", None),
        P(),
        P(("dp", "group"), None),
        P(("dp", "group"), None),
    )
    return jax.shard_map(
        local,
        mesh=mesh,
        in_specs=placed,
        out_specs=(P("dp", None), P(("dp", "group"))),
        check_vma=False,
    )
```

```python
import math

import jax
import jax.numpy as jnp
from jax import lax
from jax.experimental import pallas as pl
from jax.sharding import PartitionSpec as P


def split_dot(left, right):
    high = left.astype(jnp.bfloat16)
    low = (left - high.astype(jnp.float32)).astype(jnp.bfloat16)
    dims = (((0,), (0,)), ((), ()))
    return lax.dot_general(high, right, dims, preferred_element_type=jnp.float32) + lax.dot_general(
        low, right, dims, preferred_element_type=jnp.float32
    )


def send_kernel(ids_ref, hidden_ref, out_ref):
    hidden = hidden_ref[...]
    owners, capacity, _ = out_ref.shape
    rows = lax.broadcasted_iota(jnp.int32, (owners, hidden.shape[0]), 1)
    for slot in range(capacity):
        pick = (ids_ref[:, slot : slot + 1] == rows).astype(jnp.bfloat16)
        out_ref[:, slot, :] = jnp.dot(pick, hidden, preferred_element_type=jnp.float32).astype(
            jnp.bfloat16
        )


def local(queries, passage_hidden, out_weight, neg_owner, neg_local):
    dp_count = lax.axis_size("dp")
    group_pos = lax.axis_index("group")
    query_rows, width = queries.shape
    passage_rows = passage_hidden.shape[0]
    neg_count = neg_local.shape[1]
    ref_count = query_rows * neg_count
    capacity = 2 * ref_count // dp_count
    out_rows = out_weight.shape[0] // dp_count
    score_scale = 1.5 / math.sqrt(width)
    owners = neg_owner.reshape(ref_count)
    local_ids = neg_local.reshape(ref_count)
    ref_index = jnp.arange(ref_count, dtype=jnp.int32)
    same_owner = (owners[:, None] == owners[None, :]) & (ref_index[:, None] > ref_index[None, :])
    slot_rank = jnp.sum(same_owner.astype(jnp.int32), axis=1)
    position = owners * capacity + slot_rank
    slots = jnp.arange(dp_count * capacity, dtype=jnp.int32)
    requests = jnp.sum(
        jnp.where(position[:, None] == slots[None, :], local_ids[:, None], 0), axis=0
    ).reshape(dp_count, capacity)
    id_block = lax.all_to_all(requests, "dp", split_axis=0, concat_axis=0, tiled=True)
    hidden_block = pl.pallas_call(
        send_kernel,
        out_shape=jax.ShapeDtypeStruct((dp_count, capacity, width), jnp.bfloat16),
    )(id_block, passage_hidden)
    returned_hidden = lax.all_to_all(hidden_block, "dp", split_axis=0, concat_axis=0, tiled=True)
    pick_back = (
        position[:, None, None]
        == (jnp.arange(dp_count * capacity, dtype=jnp.int32).reshape(1, dp_count, capacity))
    ).astype(jnp.bfloat16)
    neg_hidden = jnp.einsum(
        "rkc,kcd->rd", pick_back, returned_hidden, preferred_element_type=jnp.float32
    ).astype(jnp.bfloat16)
    pos_hidden = lax.dynamic_slice_in_dim(passage_hidden, group_pos * query_rows, query_rows, 0)
    neg_keys = jnp.dot(neg_hidden, out_weight, preferred_element_type=jnp.float32).astype(
        jnp.bfloat16
    ).reshape(query_rows, neg_count, width)
    pos_keys = jnp.dot(pos_hidden, out_weight, preferred_element_type=jnp.float32).astype(
        jnp.bfloat16
    )
    pos_logit = (
        jnp.einsum("qd,qd->q", queries, pos_keys, preferred_element_type=jnp.float32) * score_scale
    )
    neg_logit = (
        jnp.einsum("qd,qjd->qj", queries, neg_keys, preferred_element_type=jnp.float32)
        * score_scale
    )
    logits = jnp.concatenate([pos_logit[:, None], neg_logit], axis=1)
    log_total = jnp.log(jnp.sum(jnp.exp(logits), axis=1))
    query_loss = log_total - pos_logit
    soft_prob = jnp.exp(logits - log_total[:, None])
    neg_coef = soft_prob[:, 1:] * score_scale
    pos_coef = (soft_prob[:, 0] - 1.0) * score_scale
    mixed = jnp.sum(
        neg_coef[:, :, None] * neg_hidden.reshape(query_rows, neg_count, width).astype(jnp.float32),
        axis=1,
    ) + pos_coef[:, None] * pos_hidden.astype(jnp.float32)
    col_half = width // 2
    swap = [(0, 1), (1, 0)]
    other_mixed = lax.ppermute(mixed, "group", swap)
    other_queries = lax.ppermute(queries, "group", swap)
    own_cols = lax.dynamic_slice_in_dim(queries, group_pos * col_half, col_half, 1)
    other_cols = lax.dynamic_slice_in_dim(other_queries, group_pos * col_half, col_half, 1)
    partial = split_dot(mixed, own_cols) + split_dot(other_mixed, other_cols)
    partial = partial.astype(jnp.bfloat16).reshape(dp_count, out_rows, col_half)
    partial = lax.all_to_all(partial, "dp", split_axis=0, concat_axis=0, tiled=True)
    weight_half = jnp.sum(partial.astype(jnp.float32), axis=0)
    other_half = lax.ppermute(weight_half, "group", swap)
    weight_grad = jnp.where(
        group_pos == 0,
        jnp.concatenate([weight_half, other_half], axis=1),
        jnp.concatenate([other_half, weight_half], axis=1),
    )
    return (weight_grad, query_loss)


def solution(mesh):
    placed = (
        P(("dp", "group"), None),
        P("dp", None),
        P(),
        P(("dp", "group"), None),
        P(("dp", "group"), None),
    )
    return jax.shard_map(
        local,
        mesh=mesh,
        in_specs=placed,
        out_specs=(P("dp", None), P(("dp", "group"))),
        check_vma=False,
    )
```

```python
import math

import jax
import jax.numpy as jnp
from jax import lax
from jax.experimental import pallas as pl
from jax.sharding import PartitionSpec as P


def split_dot(left, right):
    high = left.astype(jnp.bfloat16)
    low = (left - high.astype(jnp.float32)).astype(jnp.bfloat16)
    dims = (((0,), (0,)), ((), ()))
    return lax.dot_general(high, right, dims, preferred_element_type=jnp.float32) + lax.dot_general(
        low, right, dims, preferred_element_type=jnp.float32
    )


def send_kernel(ids_ref, hidden_ref, out_ref):
    hidden = hidden_ref[...]
    owners, capacity, _ = out_ref.shape
    rows = lax.broadcasted_iota(jnp.int32, (owners, hidden.shape[0]), 1)
    for slot in range(capacity):
        pick = (ids_ref[:, slot : slot + 1] == rows).astype(jnp.bfloat16)
        out_ref[:, slot, :] = jnp.dot(pick, hidden, preferred_element_type=jnp.float32).astype(
            jnp.bfloat16
        )


def score_kernel(neg_ref, pos_ref, q_ref, w_ref, mixed_ref, loss_ref):
    f32 = jnp.float32
    queries, width = q_ref.shape
    neg_count = neg_ref.shape[0] // queries
    scale = 1.5 / math.sqrt(width)
    w = w_ref[...]
    neg = neg_ref[...]
    keys = jnp.dot(neg, w, preferred_element_type=f32).astype(jnp.bfloat16).astype(f32)
    pos = pos_ref[...]
    pos_keys = jnp.dot(pos, w, preferred_element_type=f32).astype(jnp.bfloat16).astype(f32)
    q = q_ref[...].astype(f32)
    q3 = q.reshape(queries, 1, width)
    neg_logit = jnp.sum(keys.reshape(queries, neg_count, width) * q3, axis=2, keepdims=True) * scale
    pos_logit = jnp.sum((pos_keys * q).reshape(queries, 1, width), axis=2, keepdims=True) * scale
    total = jnp.exp(pos_logit) + jnp.sum(jnp.exp(neg_logit), axis=1, keepdims=True)
    log_total = jnp.log(total)
    neg_coef = jnp.exp(neg_logit - log_total) * scale
    pos_coef = (jnp.exp(pos_logit - log_total) - 1.0) * scale
    mixed = jnp.sum(neg.astype(f32).reshape(queries, neg_count, width) * neg_coef, axis=1, keepdims=True)
    mixed = mixed + pos_coef * pos.astype(f32).reshape(queries, 1, width)
    mixed_ref[...] = mixed.reshape(queries, width)
    loss_ref[...] = jnp.broadcast_to((log_total - pos_logit).reshape(queries, 1), loss_ref.shape)

def score(neg, pos, q, w):
    return pl.pallas_call(
        score_kernel,
        out_shape=(
            jax.ShapeDtypeStruct(q.shape, jnp.float32),
            jax.ShapeDtypeStruct((q.shape[0], 128), jnp.float32),
        ),
    )(neg, pos, q, w)


def local(queries, passage_hidden, out_weight, neg_owner, neg_local):
    dp_count = lax.axis_size("dp")
    group_pos = lax.axis_index("group")
    query_rows, width = queries.shape
    passage_rows = passage_hidden.shape[0]
    neg_count = neg_local.shape[1]
    ref_count = query_rows * neg_count
    capacity = 2 * ref_count // dp_count
    out_rows = out_weight.shape[0] // dp_count
    score_scale = 1.5 / math.sqrt(width)
    owners = neg_owner.reshape(ref_count)
    local_ids = neg_local.reshape(ref_count)
    ref_index = jnp.arange(ref_count, dtype=jnp.int32)
    same_owner = (owners[:, None] == owners[None, :]) & (ref_index[:, None] > ref_index[None, :])
    slot_rank = jnp.sum(same_owner.astype(jnp.int32), axis=1)
    position = owners * capacity + slot_rank
    slots = jnp.arange(dp_count * capacity, dtype=jnp.int32)
    requests = jnp.sum(
        jnp.where(position[:, None] == slots[None, :], local_ids[:, None], 0), axis=0
    ).reshape(dp_count, capacity)
    id_block = lax.all_to_all(requests, "dp", split_axis=0, concat_axis=0, tiled=True)
    hidden_block = pl.pallas_call(
        send_kernel,
        out_shape=jax.ShapeDtypeStruct((dp_count, capacity, width), jnp.bfloat16),
    )(id_block, passage_hidden)
    returned_hidden = lax.all_to_all(hidden_block, "dp", split_axis=0, concat_axis=0, tiled=True)
    pick_back = (
        position[:, None, None]
        == (jnp.arange(dp_count * capacity, dtype=jnp.int32).reshape(1, dp_count, capacity))
    ).astype(jnp.bfloat16)
    neg_hidden = jnp.einsum(
        "rkc,kcd->rd", pick_back, returned_hidden, preferred_element_type=jnp.float32
    ).astype(jnp.bfloat16)
    pos_hidden = lax.dynamic_slice_in_dim(passage_hidden, group_pos * query_rows, query_rows, 0)
    mixed, loss_rows = score(neg_hidden, pos_hidden, queries, out_weight)
    query_loss = loss_rows[:, 0]
    col_half = width // 2
    swap = [(0, 1), (1, 0)]
    other_mixed = lax.ppermute(mixed, "group", swap)
    other_queries = lax.ppermute(queries, "group", swap)
    own_cols = lax.dynamic_slice_in_dim(queries, group_pos * col_half, col_half, 1)
    other_cols = lax.dynamic_slice_in_dim(other_queries, group_pos * col_half, col_half, 1)
    partial = split_dot(mixed, own_cols) + split_dot(other_mixed, other_cols)
    partial = partial.astype(jnp.bfloat16).reshape(dp_count, out_rows, col_half)
    partial = lax.all_to_all(partial, "dp", split_axis=0, concat_axis=0, tiled=True)
    weight_half = jnp.sum(partial.astype(jnp.float32), axis=0)
    other_half = lax.ppermute(weight_half, "group", swap)
    weight_grad = jnp.where(
        group_pos == 0,
        jnp.concatenate([weight_half, other_half], axis=1),
        jnp.concatenate([other_half, weight_half], axis=1),
    )
    return (weight_grad, query_loss)


def solution(mesh):
    placed = (
        P(("dp", "group"), None),
        P("dp", None),
        P(),
        P(("dp", "group"), None),
        P(("dp", "group"), None),
    )
    return jax.shard_map(
        local,
        mesh=mesh,
        in_specs=placed,
        out_specs=(P("dp", None), P(("dp", "group"))),
        check_vma=False,
    )
```

```python
import math

import jax
import jax.numpy as jnp
from jax import lax
from jax.experimental import pallas as pl
from jax.sharding import PartitionSpec as P


def send_kernel(ids_ref, hidden_ref, out_ref):
    hidden = hidden_ref[...]
    owners, capacity, width = out_ref.shape
    rows = lax.broadcasted_iota(jnp.int32, (owners, capacity, hidden.shape[0]), 2)
    pick = (ids_ref[...][:, :, None] == rows).astype(jnp.bfloat16)
    picked = jnp.dot(
        pick.reshape(owners * capacity, hidden.shape[0]), hidden, preferred_element_type=jnp.float32
    )
    out_ref[...] = picked.astype(jnp.bfloat16).reshape(owners, capacity, width)


def local(queries, passage_hidden, out_weight, neg_owner, neg_local):
    dp_count = lax.axis_size("dp")
    group_pos = lax.axis_index("group")
    query_rows, width = queries.shape
    passage_rows = passage_hidden.shape[0]
    neg_count = neg_local.shape[1]
    ref_count = query_rows * neg_count
    capacity = 2 * ref_count // dp_count
    out_rows = out_weight.shape[0] // dp_count
    score_scale = 1.5 / math.sqrt(width)
    owners = neg_owner.reshape(ref_count)
    local_ids = neg_local.reshape(ref_count)
    ref_index = jnp.arange(ref_count, dtype=jnp.int32)
    same_owner = (owners[:, None] == owners[None, :]) & (ref_index[:, None] > ref_index[None, :])
    slot_rank = jnp.sum(same_owner.astype(jnp.int32), axis=1)
    position = owners * capacity + slot_rank
    slots = jnp.arange(dp_count * capacity, dtype=jnp.int32)
    requests = jnp.sum(
        jnp.where(position[:, None] == slots[None, :], local_ids[:, None], 0), axis=0
    ).reshape(dp_count, capacity)
    id_block = lax.all_to_all(requests, "dp", split_axis=0, concat_axis=0, tiled=True)
    hidden_block = pl.pallas_call(
        send_kernel,
        out_shape=jax.ShapeDtypeStruct((dp_count, capacity, width), jnp.bfloat16),
    )(id_block, passage_hidden)
    returned_hidden = lax.all_to_all(hidden_block, "dp", split_axis=0, concat_axis=0, tiled=True)
    pick_back = (
        position[:, None, None]
        == (jnp.arange(dp_count * capacity, dtype=jnp.int32).reshape(1, dp_count, capacity))
    ).astype(jnp.bfloat16)
    neg_hidden = jnp.einsum(
        "rkc,kcd->rd", pick_back, returned_hidden, preferred_element_type=jnp.float32
    ).astype(jnp.bfloat16)
    pos_hidden = lax.dynamic_slice_in_dim(passage_hidden, group_pos * query_rows, query_rows, 0)
    neg_keys = jnp.dot(neg_hidden, out_weight, preferred_element_type=jnp.float32).astype(
        jnp.bfloat16
    ).reshape(query_rows, neg_count, width)
    pos_keys = jnp.dot(pos_hidden, out_weight, preferred_element_type=jnp.float32).astype(
        jnp.bfloat16
    )
    pos_logit = (
        jnp.einsum("qd,qd->q", queries, pos_keys, preferred_element_type=jnp.float32) * score_scale
    )
    neg_logit = (
        jnp.einsum("qd,qjd->qj", queries, neg_keys, preferred_element_type=jnp.float32)
        * score_scale
    )
    logits = jnp.concatenate([pos_logit[:, None], neg_logit], axis=1)
    log_total = jnp.log(jnp.sum(jnp.exp(logits), axis=1))
    query_loss = log_total - pos_logit
    soft_prob = jnp.exp(logits - log_total[:, None])
    neg_coef = soft_prob[:, 1:] * score_scale
    pos_coef = (soft_prob[:, 0] - 1.0) * score_scale
    mixed = jnp.sum(
        neg_coef[:, :, None] * neg_hidden.reshape(query_rows, neg_count, width).astype(jnp.float32),
        axis=1,
    ) + pos_coef[:, None] * pos_hidden.astype(jnp.float32)
    col_half = width // 2
    swap = [(0, 1), (1, 0)]
    mixed_high = mixed.astype(jnp.bfloat16)
    mixed_parts = jnp.concatenate(
        [mixed_high, (mixed - mixed_high.astype(jnp.float32)).astype(jnp.bfloat16)], axis=0
    )
    other_parts = lax.ppermute(mixed_parts, "group", swap)
    other_queries = lax.ppermute(queries, "group", swap)
    own_cols = lax.dynamic_slice_in_dim(queries, group_pos * col_half, col_half, 1)
    other_cols = lax.dynamic_slice_in_dim(other_queries, group_pos * col_half, col_half, 1)
    partial = lax.dot_general(
        jnp.concatenate([mixed_parts, other_parts], axis=0),
        jnp.concatenate([own_cols, own_cols, other_cols, other_cols], axis=0),
        (((0,), (0,)), ((), ())),
        preferred_element_type=jnp.float32,
    )
    partial = partial.astype(jnp.bfloat16).reshape(dp_count, out_rows, col_half)
    partial = lax.all_to_all(partial, "dp", split_axis=0, concat_axis=0, tiled=True)
    weight_half = jnp.sum(partial.astype(jnp.float32), axis=0)
    other_half = lax.ppermute(weight_half, "group", swap)
    weight_grad = jnp.where(
        group_pos == 0,
        jnp.concatenate([weight_half, other_half], axis=1),
        jnp.concatenate([other_half, weight_half], axis=1),
    )
    return (weight_grad, query_loss)


def solution(mesh):
    placed = (
        P(("dp", "group"), None),
        P("dp", None),
        P(),
        P(("dp", "group"), None),
        P(("dp", "group"), None),
    )
    return jax.shard_map(
        local,
        mesh=mesh,
        in_specs=placed,
        out_specs=(P("dp", None), P(("dp", "group"))),
        check_vma=False,
    )
```

```python
import math

import jax
import jax.numpy as jnp
from jax import lax
from jax.experimental import pallas as pl
from jax.sharding import PartitionSpec as P


def send_kernel(ids_ref, hidden_ref, out_ref):
    hidden = hidden_ref[...]
    owners, capacity, width = out_ref.shape
    rows = lax.broadcasted_iota(jnp.int32, (owners, capacity, hidden.shape[0]), 2)
    pick = (ids_ref[...][:, :, None] == rows).astype(jnp.bfloat16)
    picked = jnp.dot(
        pick.reshape(owners * capacity, hidden.shape[0]), hidden, preferred_element_type=jnp.float32
    )
    out_ref[...] = picked.astype(jnp.bfloat16).reshape(owners, capacity, width)


def local(queries, passage_hidden, out_weight, neg_owner, neg_local):
    dp_count = lax.axis_size("dp")
    group_pos = lax.axis_index("group")
    query_rows, width = queries.shape
    passage_rows = passage_hidden.shape[0]
    neg_count = neg_local.shape[1]
    ref_count = query_rows * neg_count
    capacity = 2 * ref_count // dp_count
    out_rows = out_weight.shape[0] // dp_count
    score_scale = 1.5 / math.sqrt(width)
    owners = neg_owner.reshape(ref_count)
    local_ids = neg_local.reshape(ref_count)
    ref_index = jnp.arange(ref_count, dtype=jnp.int32)
    same_owner = (owners[:, None] == owners[None, :]) & (ref_index[:, None] > ref_index[None, :])
    own_term = jnp.where(ref_index[:, None] == ref_index[None, :], owners[:, None] * capacity, 0)
    position = jnp.sum(same_owner.astype(jnp.int32) + own_term, axis=1)
    slots = jnp.arange(dp_count * capacity, dtype=jnp.int32)
    requests = jnp.sum(
        jnp.where(position[:, None] == slots[None, :], local_ids[:, None], 0), axis=0
    ).reshape(dp_count, capacity)
    id_block = lax.all_to_all(requests, "dp", split_axis=0, concat_axis=0, tiled=True)
    hidden_block = pl.pallas_call(
        send_kernel,
        out_shape=jax.ShapeDtypeStruct((dp_count, capacity, width), jnp.bfloat16),
    )(id_block, passage_hidden)
    returned_hidden = lax.all_to_all(hidden_block, "dp", split_axis=0, concat_axis=0, tiled=True)
    pick_back = (
        position[:, None, None]
        == (jnp.arange(dp_count * capacity, dtype=jnp.int32).reshape(1, dp_count, capacity))
    ).astype(jnp.bfloat16)
    neg_hidden = jnp.einsum(
        "rkc,kcd->rd", pick_back, returned_hidden, preferred_element_type=jnp.float32
    ).astype(jnp.bfloat16)
    pos_hidden = lax.dynamic_slice_in_dim(passage_hidden, group_pos * query_rows, query_rows, 0)
    neg_keys = jnp.dot(neg_hidden, out_weight, preferred_element_type=jnp.float32).astype(
        jnp.bfloat16
    ).reshape(query_rows, neg_count, width)
    pos_keys = jnp.dot(pos_hidden, out_weight, preferred_element_type=jnp.float32).astype(
        jnp.bfloat16
    )
    pos_logit = (
        jnp.einsum("qd,qd->q", queries, pos_keys, preferred_element_type=jnp.float32) * score_scale
    )
    neg_logit = (
        jnp.einsum("qd,qjd->qj", queries, neg_keys, preferred_element_type=jnp.float32)
        * score_scale
    )
    logits = jnp.concatenate([pos_logit[:, None], neg_logit], axis=1)
    log_total = jnp.log(jnp.sum(jnp.exp(logits), axis=1))
    query_loss = log_total - pos_logit
    soft_prob = jnp.exp(logits - log_total[:, None])
    neg_coef = soft_prob[:, 1:] * score_scale
    pos_coef = (soft_prob[:, 0] - 1.0) * score_scale
    mixed = jnp.sum(
        neg_coef[:, :, None] * neg_hidden.reshape(query_rows, neg_count, width).astype(jnp.float32),
        axis=1,
    ) + pos_coef[:, None] * pos_hidden.astype(jnp.float32)
    col_half = width // 2
    swap = [(0, 1), (1, 0)]
    mixed_high = mixed.astype(jnp.bfloat16)
    mixed_parts = jnp.concatenate(
        [mixed_high, (mixed - mixed_high.astype(jnp.float32)).astype(jnp.bfloat16)], axis=0
    )
    other_parts = lax.ppermute(mixed_parts, "group", swap)
    other_queries = lax.ppermute(queries, "group", swap)
    own_cols = lax.dynamic_slice_in_dim(queries, group_pos * col_half, col_half, 1)
    other_cols = lax.dynamic_slice_in_dim(other_queries, group_pos * col_half, col_half, 1)
    partial = lax.dot_general(
        jnp.concatenate([mixed_parts, other_parts], axis=0),
        jnp.concatenate([own_cols, own_cols, other_cols, other_cols], axis=0),
        (((0,), (0,)), ((), ())),
        preferred_element_type=jnp.float32,
    )
    partial = partial.astype(jnp.bfloat16).reshape(dp_count, out_rows, col_half)
    partial = lax.all_to_all(partial, "dp", split_axis=0, concat_axis=0, tiled=True)
    weight_half = jnp.sum(partial.astype(jnp.float32), axis=0)
    other_half = lax.ppermute(weight_half, "group", swap)
    weight_grad = jnp.where(
        group_pos == 0,
        jnp.concatenate([weight_half, other_half], axis=1),
        jnp.concatenate([other_half, weight_half], axis=1),
    )
    return (weight_grad, query_loss)


def solution(mesh):
    placed = (
        P(("dp", "group"), None),
        P("dp", None),
        P(),
        P(("dp", "group"), None),
        P(("dp", "group"), None),
    )
    return jax.shard_map(
        local,
        mesh=mesh,
        in_specs=placed,
        out_specs=(P("dp", None), P(("dp", "group"))),
        check_vma=False,
    )
```

```python
import math

import jax
import jax.numpy as jnp
from jax import lax
from jax.experimental import pallas as pl
from jax.sharding import PartitionSpec as P


def send_kernel(ids_ref, hidden_ref, out_ref):
    hidden = hidden_ref[...]
    owners, capacity, width = out_ref.shape
    rows = lax.broadcasted_iota(jnp.int32, (owners, capacity, hidden.shape[0]), 2)
    pick = (ids_ref[...][:, :, None] == rows).astype(jnp.bfloat16)
    picked = jnp.dot(
        pick.reshape(owners * capacity, hidden.shape[0]), hidden, preferred_element_type=jnp.float32
    )
    out_ref[...] = picked.astype(jnp.bfloat16).reshape(owners, capacity, width)


def local(queries, passage_hidden, out_weight, neg_owner, neg_local):
    dp_count = lax.axis_size("dp")
    group_pos = lax.axis_index("group")
    query_rows, width = queries.shape
    passage_rows = passage_hidden.shape[0]
    neg_count = neg_local.shape[1]
    ref_count = query_rows * neg_count
    capacity = 2 * ref_count // dp_count
    out_rows = out_weight.shape[0] // dp_count
    score_scale = 1.5 / math.sqrt(width)
    owners = neg_owner.reshape(ref_count)
    local_ids = neg_local.reshape(ref_count)
    ref_index = jnp.arange(ref_count, dtype=jnp.int32)
    same_owner = (owners[:, None] == owners[None, :]) & (ref_index[:, None] > ref_index[None, :])
    slot_rank = jnp.sum(same_owner.astype(jnp.int32), axis=1)
    position = owners * capacity + slot_rank
    slots = jnp.arange(dp_count * capacity, dtype=jnp.int32)
    requests = jnp.sum(
        jnp.where(position[:, None] == slots[None, :], local_ids[:, None], 0), axis=0
    ).reshape(dp_count, capacity)
    id_block = lax.all_to_all(requests, "dp", split_axis=0, concat_axis=0, tiled=True)
    hidden_block = pl.pallas_call(
        send_kernel,
        out_shape=jax.ShapeDtypeStruct((dp_count, capacity, width), jnp.bfloat16),
    )(id_block, passage_hidden)
    returned_hidden = lax.all_to_all(hidden_block, "dp", split_axis=0, concat_axis=0, tiled=True)
    pick_back = (
        position[:, None, None]
        == (jnp.arange(dp_count * capacity, dtype=jnp.int32).reshape(1, dp_count, capacity))
    ).astype(jnp.bfloat16)
    pick_back = lax.optimization_barrier(pick_back)
    neg_hidden = jnp.einsum(
        "rkc,kcd->rd", pick_back, returned_hidden, preferred_element_type=jnp.float32
    ).astype(jnp.bfloat16)
    pos_hidden = lax.dynamic_slice_in_dim(passage_hidden, group_pos * query_rows, query_rows, 0)
    neg_keys = jnp.dot(neg_hidden, out_weight, preferred_element_type=jnp.float32).astype(
        jnp.bfloat16
    ).reshape(query_rows, neg_count, width)
    pos_keys = jnp.dot(pos_hidden, out_weight, preferred_element_type=jnp.float32).astype(
        jnp.bfloat16
    )
    pos_logit = (
        jnp.einsum("qd,qd->q", queries, pos_keys, preferred_element_type=jnp.float32) * score_scale
    )
    neg_logit = (
        jnp.einsum("qd,qjd->qj", queries, neg_keys, preferred_element_type=jnp.float32)
        * score_scale
    )
    logits = jnp.concatenate([pos_logit[:, None], neg_logit], axis=1)
    log_total = jnp.log(jnp.sum(jnp.exp(logits), axis=1))
    query_loss = log_total - pos_logit
    soft_prob = jnp.exp(logits - log_total[:, None])
    neg_coef = soft_prob[:, 1:] * score_scale
    pos_coef = (soft_prob[:, 0] - 1.0) * score_scale
    mixed = jnp.sum(
        neg_coef[:, :, None] * neg_hidden.reshape(query_rows, neg_count, width).astype(jnp.float32),
        axis=1,
    ) + pos_coef[:, None] * pos_hidden.astype(jnp.float32)
    col_half = width // 2
    swap = [(0, 1), (1, 0)]
    mixed_high = mixed.astype(jnp.bfloat16)
    mixed_parts = jnp.concatenate(
        [mixed_high, (mixed - mixed_high.astype(jnp.float32)).astype(jnp.bfloat16)], axis=0
    )
    other_parts = lax.ppermute(mixed_parts, "group", swap)
    other_queries = lax.ppermute(queries, "group", swap)
    own_cols = lax.dynamic_slice_in_dim(queries, group_pos * col_half, col_half, 1)
    other_cols = lax.dynamic_slice_in_dim(other_queries, group_pos * col_half, col_half, 1)
    partial = lax.dot_general(
        jnp.concatenate([mixed_parts, other_parts], axis=0),
        jnp.concatenate([own_cols, own_cols, other_cols, other_cols], axis=0),
        (((0,), (0,)), ((), ())),
        preferred_element_type=jnp.float32,
    )
    partial = partial.astype(jnp.bfloat16).reshape(dp_count, out_rows, col_half)
    partial = lax.all_to_all(partial, "dp", split_axis=0, concat_axis=0, tiled=True)
    weight_half = jnp.sum(partial.astype(jnp.float32), axis=0)
    other_half = lax.ppermute(weight_half, "group", swap)
    weight_grad = jnp.where(
        group_pos == 0,
        jnp.concatenate([weight_half, other_half], axis=1),
        jnp.concatenate([other_half, weight_half], axis=1),
    )
    return (weight_grad, query_loss)


def solution(mesh):
    placed = (
        P(("dp", "group"), None),
        P("dp", None),
        P(),
        P(("dp", "group"), None),
        P(("dp", "group"), None),
    )
    return jax.shard_map(
        local,
        mesh=mesh,
        in_specs=placed,
        out_specs=(P("dp", None), P(("dp", "group"))),
        check_vma=False,
    )
```

```python
import math

import jax
import jax.numpy as jnp
from jax import lax
from jax.experimental import pallas as pl
from jax.sharding import PartitionSpec as P


def send_kernel(ids_ref, hidden_ref, out_ref):
    hidden = hidden_ref[...]
    owners, capacity, width = out_ref.shape
    rows = lax.broadcasted_iota(jnp.int32, (owners, capacity, hidden.shape[0]), 2)
    pick = (ids_ref[...][:, :, None] == rows).astype(jnp.bfloat16)
    picked = jnp.dot(
        pick.reshape(owners * capacity, hidden.shape[0]), hidden, preferred_element_type=jnp.float32
    )
    out_ref[...] = picked.astype(jnp.bfloat16).reshape(owners, capacity, width)


def local(queries, passage_hidden, out_weight, neg_owner, neg_local):
    dp_count = lax.axis_size("dp")
    group_pos = lax.axis_index("group")
    query_rows, width = queries.shape
    passage_rows = passage_hidden.shape[0]
    neg_count = neg_local.shape[1]
    ref_count = query_rows * neg_count
    capacity = 2 * ref_count // dp_count
    out_rows = out_weight.shape[0] // dp_count
    score_scale = 1.5 / math.sqrt(width)
    owners = neg_owner.reshape(ref_count)
    local_ids = neg_local.reshape(ref_count)
    ref_index = jnp.arange(ref_count, dtype=jnp.int32)
    same_owner = (owners[:, None] == owners[None, :]) & (ref_index[:, None] > ref_index[None, :])
    slot_rank = jnp.sum(same_owner.astype(jnp.int32), axis=1)
    position = owners * capacity + slot_rank
    slots = jnp.arange(dp_count * capacity, dtype=jnp.int32)
    requests = jnp.sum(
        jnp.where(position[:, None] == slots[None, :], local_ids[:, None], 0), axis=0
    ).reshape(dp_count, capacity)
    id_block = lax.all_to_all(requests, "dp", split_axis=0, concat_axis=0, tiled=True)
    hidden_block = pl.pallas_call(
        send_kernel,
        out_shape=jax.ShapeDtypeStruct((dp_count, capacity, width), jnp.bfloat16),
    )(id_block, passage_hidden)
    returned_hidden = lax.all_to_all(hidden_block, "dp", split_axis=0, concat_axis=0, tiled=True)
    pick_back = (
        position[:, None, None]
        == (jnp.arange(dp_count * capacity, dtype=jnp.int32).reshape(1, dp_count, capacity))
    ).astype(jnp.bfloat16)
    neg_hidden = jnp.einsum(
        "rkc,kcd->rd", pick_back, returned_hidden, preferred_element_type=jnp.float32
    ).astype(jnp.bfloat16)
    pos_hidden = lax.dynamic_slice_in_dim(passage_hidden, group_pos * query_rows, query_rows, 0)
    neg_keys = jnp.dot(neg_hidden, out_weight, preferred_element_type=jnp.float32).astype(
        jnp.bfloat16
    ).reshape(query_rows, neg_count, width)
    pos_keys = jnp.dot(pos_hidden, out_weight, preferred_element_type=jnp.float32).astype(
        jnp.bfloat16
    )
    pos_logit = (
        jnp.einsum("qd,qd->q", queries, pos_keys, preferred_element_type=jnp.float32) * score_scale
    )
    neg_logit = (
        jnp.einsum("qd,qjd->qj", queries, neg_keys, preferred_element_type=jnp.float32)
        * score_scale
    )
    logits = jnp.concatenate([pos_logit[:, None], neg_logit], axis=1)
    log_total = jnp.log(jnp.sum(jnp.exp(logits), axis=1))
    query_loss = log_total - pos_logit
    soft_prob = jnp.exp(logits - log_total[:, None])
    neg_coef = soft_prob[:, 1:] * score_scale
    pos_coef = (soft_prob[:, 0] - 1.0) * score_scale
    mixed = jnp.sum(
        neg_coef[:, :, None] * neg_hidden.reshape(query_rows, neg_count, width).astype(jnp.float32),
        axis=1,
    ) + pos_coef[:, None] * pos_hidden.astype(jnp.float32)
    col_half = width // 2
    swap = [(0, 1), (1, 0)]
    mixed_high = mixed.astype(jnp.bfloat16)
    mixed_parts = jnp.concatenate(
        [mixed_high, (mixed - mixed_high.astype(jnp.float32)).astype(jnp.bfloat16)], axis=0
    )
    other_parts = lax.ppermute(mixed_parts, "group", swap)
    other_queries = lax.ppermute(queries, "group", swap)
    own_cols = lax.dynamic_slice_in_dim(queries, group_pos * col_half, col_half, 1)
    other_cols = lax.dynamic_slice_in_dim(other_queries, group_pos * col_half, col_half, 1)
    partial = lax.dot_general(
        jnp.concatenate([mixed_parts, other_parts], axis=0),
        jnp.concatenate([own_cols, own_cols, other_cols, other_cols], axis=0),
        (((0,), (0,)), ((), ())),
        preferred_element_type=jnp.float32,
    )
    partial = partial.astype(jnp.bfloat16).reshape(dp_count, out_rows // 2, 2 * col_half)
    partial = lax.all_to_all(partial, "dp", split_axis=0, concat_axis=0, tiled=True)
    weight_half = jnp.sum(partial.astype(jnp.float32), axis=0).reshape(out_rows, col_half)
    other_half = lax.ppermute(weight_half, "group", swap)
    weight_grad = jnp.where(
        group_pos == 0,
        jnp.concatenate([weight_half, other_half], axis=1),
        jnp.concatenate([other_half, weight_half], axis=1),
    )
    return (weight_grad, query_loss)


def solution(mesh):
    placed = (
        P(("dp", "group"), None),
        P("dp", None),
        P(),
        P(("dp", "group"), None),
        P(("dp", "group"), None),
    )
    return jax.shard_map(
        local,
        mesh=mesh,
        in_specs=placed,
        out_specs=(P("dp", None), P(("dp", "group"))),
        check_vma=False,
    )
```

```python
import math

import jax
import jax.numpy as jnp
from jax import lax
from jax.experimental import pallas as pl
from jax.sharding import PartitionSpec as P


def send_kernel(ids_ref, hidden_ref, out_ref):
    hidden = hidden_ref[...]
    owners, capacity, width = out_ref.shape
    rows = lax.broadcasted_iota(jnp.int32, (owners, capacity, hidden.shape[0]), 2)
    pick = (ids_ref[...][:, :, None] == rows).astype(jnp.bfloat16)
    picked = jnp.dot(
        pick.reshape(owners * capacity, hidden.shape[0]), hidden, preferred_element_type=jnp.float32
    )
    out_ref[...] = picked.astype(jnp.bfloat16).reshape(owners, capacity, width)


def local(queries, passage_hidden, out_weight, neg_owner, neg_local):
    dp_count = lax.axis_size("dp")
    group_pos = lax.axis_index("group")
    query_rows, width = queries.shape
    passage_rows = passage_hidden.shape[0]
    neg_count = neg_local.shape[1]
    ref_count = query_rows * neg_count
    capacity = 2 * ref_count // dp_count
    out_rows = out_weight.shape[0] // dp_count
    score_scale = 1.5 / math.sqrt(width)
    owners = neg_owner.reshape(ref_count)
    local_ids = neg_local.reshape(ref_count)
    ref_index = jnp.arange(ref_count, dtype=jnp.int32)
    same_owner = (owners[:, None] == owners[None, :]) & (ref_index[:, None] > ref_index[None, :])
    slot_rank = jnp.sum(same_owner.astype(jnp.int32), axis=1)
    position = owners * capacity + slot_rank
    slots = jnp.arange(dp_count * capacity, dtype=jnp.int32)
    requests = jnp.sum(
        jnp.where(position[:, None] == slots[None, :], local_ids[:, None], 0), axis=0
    ).reshape(dp_count, capacity)
    id_block = lax.all_to_all(requests, "dp", split_axis=0, concat_axis=0, tiled=True)
    hidden_block = pl.pallas_call(
        send_kernel,
        out_shape=jax.ShapeDtypeStruct((dp_count, capacity, width), jnp.bfloat16),
    )(id_block, passage_hidden)
    returned_hidden = lax.all_to_all(hidden_block, "dp", split_axis=0, concat_axis=0, tiled=True)
    pick_back = (
        position[:, None, None]
        == (jnp.arange(dp_count * capacity, dtype=jnp.int32).reshape(1, dp_count, capacity))
    ).astype(jnp.bfloat16)
    neg_hidden = jnp.einsum(
        "rkc,kcd->rd", pick_back, returned_hidden, preferred_element_type=jnp.float32
    ).astype(jnp.bfloat16)
    pos_hidden = lax.dynamic_slice_in_dim(passage_hidden, group_pos * query_rows, query_rows, 0)
    neg_keys = jnp.dot(neg_hidden, out_weight, preferred_element_type=jnp.float32).astype(
        jnp.bfloat16
    ).reshape(query_rows, neg_count, width)
    pos_keys = jnp.dot(pos_hidden, out_weight, preferred_element_type=jnp.float32).astype(
        jnp.bfloat16
    )
    pos_logit = (
        jnp.einsum("qd,qd->q", queries, pos_keys, preferred_element_type=jnp.float32) * score_scale
    )
    neg_logit = (
        jnp.einsum("qd,qjd->qj", queries, neg_keys, preferred_element_type=jnp.float32)
        * score_scale
    )
    pos_exp = jnp.exp(pos_logit)
    neg_exp = jnp.exp(neg_logit)
    total = pos_exp + jnp.sum(neg_exp, axis=1)
    query_loss = jnp.log(total) - pos_logit
    scaled = score_scale / total
    neg_coef = neg_exp * scaled[:, None]
    pos_coef = pos_exp * scaled - score_scale
    mixed = jnp.sum(
        neg_coef[:, :, None] * neg_hidden.reshape(query_rows, neg_count, width).astype(jnp.float32),
        axis=1,
    ) + pos_coef[:, None] * pos_hidden.astype(jnp.float32)
    col_half = width // 2
    swap = [(0, 1), (1, 0)]
    mixed_high = mixed.astype(jnp.bfloat16)
    mixed_parts = jnp.concatenate(
        [mixed_high, (mixed - mixed_high.astype(jnp.float32)).astype(jnp.bfloat16)], axis=0
    )
    other_parts = lax.ppermute(mixed_parts, "group", swap)
    other_queries = lax.ppermute(queries, "group", swap)
    own_cols = lax.dynamic_slice_in_dim(queries, group_pos * col_half, col_half, 1)
    other_cols = lax.dynamic_slice_in_dim(other_queries, group_pos * col_half, col_half, 1)
    partial = lax.dot_general(
        jnp.concatenate([mixed_parts, other_parts], axis=0),
        jnp.concatenate([own_cols, own_cols, other_cols, other_cols], axis=0),
        (((0,), (0,)), ((), ())),
        preferred_element_type=jnp.float32,
    )
    partial = partial.astype(jnp.bfloat16).reshape(dp_count, out_rows, col_half)
    partial = lax.all_to_all(partial, "dp", split_axis=0, concat_axis=0, tiled=True)
    weight_half = jnp.sum(partial.astype(jnp.float32), axis=0)
    other_half = lax.ppermute(weight_half, "group", swap)
    weight_grad = jnp.where(
        group_pos == 0,
        jnp.concatenate([weight_half, other_half], axis=1),
        jnp.concatenate([other_half, weight_half], axis=1),
    )
    return (weight_grad, query_loss)


def solution(mesh):
    placed = (
        P(("dp", "group"), None),
        P("dp", None),
        P(),
        P(("dp", "group"), None),
        P(("dp", "group"), None),
    )
    return jax.shard_map(
        local,
        mesh=mesh,
        in_specs=placed,
        out_specs=(P("dp", None), P(("dp", "group"))),
        check_vma=False,
    )
```

```python
import math

import jax
import jax.numpy as jnp
from jax import lax
from jax.experimental import pallas as pl
from jax.sharding import PartitionSpec as P


def send_kernel(ids_ref, hidden_ref, out_ref):
    hidden = hidden_ref[...]
    owners, capacity, width = out_ref.shape
    rows = lax.broadcasted_iota(jnp.int32, (owners, capacity, hidden.shape[0]), 2)
    pick = (ids_ref[...][:, :, None] == rows).astype(jnp.bfloat16)
    picked = jnp.dot(
        pick.reshape(owners * capacity, hidden.shape[0]), hidden, preferred_element_type=jnp.float32
    )
    out_ref[...] = picked.astype(jnp.bfloat16).reshape(owners, capacity, width)


def local(queries, passage_hidden, out_weight, neg_owner, neg_local):
    dp_count = lax.axis_size("dp")
    group_pos = lax.axis_index("group")
    query_rows, width = queries.shape
    passage_rows = passage_hidden.shape[0]
    neg_count = neg_local.shape[1]
    ref_count = query_rows * neg_count
    capacity = 2 * ref_count // dp_count
    out_rows = out_weight.shape[0] // dp_count
    score_scale = 1.5 / math.sqrt(width)
    owners = neg_owner.reshape(ref_count)
    local_ids = neg_local.reshape(ref_count)
    ref_index = jnp.arange(ref_count, dtype=jnp.int32)
    same_owner = (owners[:, None] == owners[None, :]) & (ref_index[:, None] > ref_index[None, :])
    slot_rank = jnp.sum(same_owner.astype(jnp.int32), axis=1)
    position = owners * capacity + slot_rank
    slots = jnp.arange(dp_count * capacity, dtype=jnp.int32)
    requests = jnp.sum(
        jnp.where(position[:, None] == slots[None, :], local_ids[:, None], 0), axis=0
    ).reshape(dp_count, capacity)
    id_block = lax.all_to_all(requests, "dp", split_axis=0, concat_axis=0, tiled=True)
    hidden_block = pl.pallas_call(
        send_kernel,
        out_shape=jax.ShapeDtypeStruct((dp_count, capacity, width), jnp.bfloat16),
    )(id_block, passage_hidden)
    returned_hidden = lax.all_to_all(hidden_block, "dp", split_axis=0, concat_axis=0, tiled=True)
    pick_back = (
        position[:, None, None]
        == (jnp.arange(dp_count * capacity, dtype=jnp.int32).reshape(1, dp_count, capacity))
    ).astype(jnp.bfloat16)
    pick_back = lax.optimization_barrier(pick_back)
    neg_hidden = jnp.einsum(
        "rkc,kcd->rd", pick_back, returned_hidden, preferred_element_type=jnp.float32
    ).astype(jnp.bfloat16)
    pos_hidden = lax.dynamic_slice_in_dim(passage_hidden, group_pos * query_rows, query_rows, 0)
    neg_keys = jnp.dot(neg_hidden, out_weight, preferred_element_type=jnp.float32).astype(
        jnp.bfloat16
    ).reshape(query_rows, neg_count, width)
    pos_keys = jnp.dot(pos_hidden, out_weight, preferred_element_type=jnp.float32).astype(
        jnp.bfloat16
    )
    pos_logit = (
        jnp.einsum("qd,qd->q", queries, pos_keys, preferred_element_type=jnp.float32) * score_scale
    )
    neg_logit = (
        jnp.einsum("qd,qjd->qj", queries, neg_keys, preferred_element_type=jnp.float32)
        * score_scale
    )
    pos_exp = jnp.exp(pos_logit)
    neg_exp = jnp.exp(neg_logit)
    total = pos_exp + jnp.sum(neg_exp, axis=1)
    query_loss = jnp.log(total) - pos_logit
    scaled = score_scale / total
    neg_coef = neg_exp * scaled[:, None]
    pos_coef = pos_exp * scaled - score_scale
    mixed = jnp.sum(
        neg_coef[:, :, None] * neg_hidden.reshape(query_rows, neg_count, width).astype(jnp.float32),
        axis=1,
    ) + pos_coef[:, None] * pos_hidden.astype(jnp.float32)
    col_half = width // 2
    swap = [(0, 1), (1, 0)]
    mixed_high = mixed.astype(jnp.bfloat16)
    mixed_parts = jnp.concatenate(
        [mixed_high, (mixed - mixed_high.astype(jnp.float32)).astype(jnp.bfloat16)], axis=0
    )
    other_parts = lax.ppermute(mixed_parts, "group", swap)
    other_queries = lax.ppermute(queries, "group", swap)
    own_cols = lax.dynamic_slice_in_dim(queries, group_pos * col_half, col_half, 1)
    other_cols = lax.dynamic_slice_in_dim(other_queries, group_pos * col_half, col_half, 1)
    partial = lax.dot_general(
        jnp.concatenate([mixed_parts, other_parts], axis=0),
        jnp.concatenate([own_cols, own_cols, other_cols, other_cols], axis=0),
        (((0,), (0,)), ((), ())),
        preferred_element_type=jnp.float32,
    )
    partial = partial.astype(jnp.bfloat16).reshape(dp_count, out_rows, col_half)
    partial = lax.all_to_all(partial, "dp", split_axis=0, concat_axis=0, tiled=True)
    weight_half = jnp.sum(partial.astype(jnp.float32), axis=0)
    other_half = lax.ppermute(weight_half, "group", swap)
    weight_grad = jnp.where(
        group_pos == 0,
        jnp.concatenate([weight_half, other_half], axis=1),
        jnp.concatenate([other_half, weight_half], axis=1),
    )
    return (weight_grad, query_loss)


def solution(mesh):
    placed = (
        P(("dp", "group"), None),
        P("dp", None),
        P(),
        P(("dp", "group"), None),
        P(("dp", "group"), None),
    )
    return jax.shard_map(
        local,
        mesh=mesh,
        in_specs=placed,
        out_specs=(P("dp", None), P(("dp", "group"))),
        check_vma=False,
    )
```

```python
import math

import jax
import jax.numpy as jnp
from jax import lax
from jax.experimental import pallas as pl
from jax.sharding import PartitionSpec as P


def send_kernel(ids_ref, hidden_ref, out_ref):
    hidden = hidden_ref[...]
    owners, capacity, width = out_ref.shape
    rows = lax.broadcasted_iota(jnp.int32, (owners, capacity, hidden.shape[0]), 2)
    pick = (ids_ref[...][:, :, None] == rows).astype(jnp.bfloat16)
    picked = jnp.dot(
        pick.reshape(owners * capacity, hidden.shape[0]), hidden, preferred_element_type=jnp.float32
    )
    out_ref[...] = picked.astype(jnp.bfloat16).reshape(owners, capacity, width)


def local(queries, passage_hidden, out_weight, neg_owner, neg_local):
    dp_count = lax.axis_size("dp")
    group_pos = lax.axis_index("group")
    query_rows, width = queries.shape
    passage_rows = passage_hidden.shape[0]
    neg_count = neg_local.shape[1]
    ref_count = query_rows * neg_count
    capacity = 2 * ref_count // dp_count
    out_rows = out_weight.shape[0] // dp_count
    score_scale = 1.5 / math.sqrt(width)
    owners = neg_owner.reshape(ref_count)
    local_ids = neg_local.reshape(ref_count)
    ref_index = jnp.arange(ref_count, dtype=jnp.int32)
    same_owner = (owners[:, None] == owners[None, :]) & (ref_index[:, None] > ref_index[None, :])
    slot_rank = jnp.sum(same_owner.astype(jnp.int32), axis=1)
    position = owners * capacity + slot_rank
    slots = jnp.arange(dp_count * capacity, dtype=jnp.int32)
    requests = jnp.sum(
        jnp.where(position[:, None] == slots[None, :], local_ids[:, None], 0), axis=0
    ).reshape(dp_count, capacity)
    id_block = lax.all_to_all(requests, "dp", split_axis=0, concat_axis=0, tiled=True)
    hidden_block = pl.pallas_call(
        send_kernel,
        out_shape=jax.ShapeDtypeStruct((dp_count, capacity, width), jnp.bfloat16),
    )(id_block, passage_hidden)
    returned_hidden = lax.all_to_all(hidden_block, "dp", split_axis=0, concat_axis=0, tiled=True)
    pick_back = (
        position[:, None, None]
        == (jnp.arange(dp_count * capacity, dtype=jnp.int32).reshape(1, dp_count, capacity))
    ).astype(jnp.bfloat16)
    neg_hidden = jnp.einsum(
        "rkc,kcd->rd", pick_back, returned_hidden, preferred_element_type=jnp.float32
    ).astype(jnp.bfloat16)
    pos_hidden = lax.dynamic_slice_in_dim(passage_hidden, group_pos * query_rows, query_rows, 0)
    neg_keys = jnp.dot(neg_hidden, out_weight, preferred_element_type=jnp.float32).astype(
        jnp.bfloat16
    ).reshape(query_rows, neg_count, width)
    pos_keys = jnp.dot(pos_hidden, out_weight, preferred_element_type=jnp.float32).astype(
        jnp.bfloat16
    )
    pos_logit = (
        jnp.einsum("qd,qd->q", queries, pos_keys, preferred_element_type=jnp.float32) * score_scale
    )
    neg_logit = (
        jnp.einsum("qd,qjd->qj", queries, neg_keys, preferred_element_type=jnp.float32)
        * score_scale
    )
    logits = jnp.concatenate([pos_logit[:, None], neg_logit], axis=1)
    log_total = jnp.log(jnp.sum(jnp.exp(logits), axis=1))
    soft_prob = jnp.exp(logits - log_total[:, None])
    neg_coef = soft_prob[:, 1:] * score_scale
    pos_coef = (soft_prob[:, 0] - 1.0) * score_scale
    mixed = jnp.sum(
        neg_coef[:, :, None] * neg_hidden.reshape(query_rows, neg_count, width).astype(jnp.float32),
        axis=1,
    ) + pos_coef[:, None] * pos_hidden.astype(jnp.float32)
    col_half = width // 2
    swap = [(0, 1), (1, 0)]
    mixed_high = mixed.astype(jnp.bfloat16)
    mixed_parts = jnp.concatenate(
        [mixed_high, (mixed - mixed_high.astype(jnp.float32)).astype(jnp.bfloat16)], axis=0
    )
    other_parts = lax.ppermute(mixed_parts, "group", swap)
    other_queries = lax.ppermute(queries, "group", swap)
    own_cols = lax.dynamic_slice_in_dim(queries, group_pos * col_half, col_half, 1)
    other_cols = lax.dynamic_slice_in_dim(other_queries, group_pos * col_half, col_half, 1)
    partial = lax.dot_general(
        jnp.concatenate([mixed_parts, other_parts], axis=0),
        jnp.concatenate([own_cols, own_cols, other_cols, other_cols], axis=0),
        (((0,), (0,)), ((), ())),
        preferred_element_type=jnp.float32,
    )
    partial = partial.astype(jnp.bfloat16).reshape(dp_count, out_rows, col_half)
    partial = lax.all_to_all(partial, "dp", split_axis=0, concat_axis=0, tiled=True)
    weight_half = jnp.sum(partial.astype(jnp.float32), axis=0)
    weight_half, log_total, pos_logit = lax.optimization_barrier((weight_half, log_total, pos_logit))
    query_loss = log_total - pos_logit
    other_half = lax.ppermute(weight_half, "group", swap)
    weight_grad = jnp.where(
        group_pos == 0,
        jnp.concatenate([weight_half, other_half], axis=1),
        jnp.concatenate([other_half, weight_half], axis=1),
    )
    return (weight_grad, query_loss)


def solution(mesh):
    placed = (
        P(("dp", "group"), None),
        P("dp", None),
        P(),
        P(("dp", "group"), None),
        P(("dp", "group"), None),
    )
    return jax.shard_map(
        local,
        mesh=mesh,
        in_specs=placed,
        out_specs=(P("dp", None), P(("dp", "group"))),
        check_vma=False,
    )
```
